512 devices in a mesh: ply: 8 (over y_lo, x), tile: 64 (over z, y_hi, core).
Axes of the slice: x: 4, y: 8 (y_hi: 4, y_lo: 2; y = y_hi * 2 + y_lo), z: 8, core: 2. Of those that a mesh axis runs over, the one named last changes fastest.
Arguments:
- strain: float32 [4, 3, 16, 16384], P(None, None, None, 'tile'), may hold values from -6 to 6
- case_ids: int32 [4], replicated, may hold values from 0 to 3, each once
- angle_ids: int32 [192], P('ply'), may hold values from 0 to 3
- stiffening: float32 [192, 16, 16384], P('ply', None, 'tile'), may hold values from 0.5 to 8
- interface: float32 [192, 16, 16384], P('ply', None, 'tile'), may hold values from 0.5 to 4
Outputs:
- adjoint: float32 [4, 192, 16, 16384], P(None, 'ply', None, 'tile')
- through: float32 [192, 16, 16384], P('ply', None, 'tile')
The draws below stay inside these ranges and needn't reach their ends.
Inputs may be any that keep to these rules, and one draw needn't show every extreme that they name: `case_ids`: each of the 4 load states is taken by exactly one load case.
All inputs are finite; a program needn't handle non-finite values.
Results may differ from the reference program's by a relative error of at most 0.0085.
Values sent between devices are 32-bit elements; how exact they have to be, the bound alone decides.
No kernel may reach another device: no remote copies, remote signals or barrier semaphores. Data moves between devices by JAX's collectives and lax.ppermute only.
A program may use at most 64 MiB of HBM per device.

```python
import math
import jax
import jax.numpy as jnp
from jax import lax

ROWS = 16
CASES = 4
ITERS = 4
PLIES = 192
COLS = 16384


def touch_ends(result, stream_key, low, top_value):
    shape = result.shape
    index_at = [jax.random.randint(jax.random.fold_in(stream_key, axis), (), 0, shape[axis]) for axis in range(len(shape))]
    result = result.at[tuple(index_at)].set(low)
    longest = shape.index(max(shape))
    index_at[longest] = (index_at[longest] + 1) % shape[longest]
    return result.at[tuple(index_at)].set(top_value)


def shard_levels(rng, shape, pieces, low, top_value):
    level = 1.0
    for dim, parts in pieces:
        steps = jax.random.uniform(jax.random.fold_in(jax.random.fold_in(rng, 6), dim), (parts,), jnp.float32, low / len(pieces), top_value / len(pieces))
        level = level * jnp.repeat(jnp.exp(steps), shape[dim] // parts).reshape((-1,) + (1,) * (len(shape) - 1 - dim))
    return level


def noise(key, shape, width, reach, cuts=(), kind=jnp.bfloat16):
    loudness = shard_levels(key, shape, cuts, -0.22, 0.18) if cuts else 1.0
    values = jax.random.normal(key, shape, jnp.float32) * width * loudness
    return jnp.minimum(jnp.maximum(values, -reach), reach).astype(kind)


def setup_inputs(seed: int = 0) -> dict:
    key_list = jax.random.split(jax.random.key(seed), 6)
    return {
        "strain": noise(key_list[0], (CASES, 3, ROWS, COLS), 1.0, 6.0, ((3, 64),), jnp.float32),
        "case_ids": jax.random.permutation(key_list[1], CASES).astype(jnp.int32),
        "angle_ids": touch_ends(jax.random.randint(key_list[2], (PLIES,), 0, 4), jax.random.fold_in(key_list[2], 1), 0, 3).astype(jnp.int32),
        "stiffening": jnp.clip(jnp.exp(math.log(8.0) - 2.7725887 * jax.random.uniform(key_list[3], (PLIES, ROWS, COLS), jnp.float32) ** shard_levels(key_list[3], (PLIES, ROWS, COLS), ((0, 8), (2, 64)), -0.2, 0.2)), 0.5, 8.0),
        "interface": jnp.clip(jnp.exp(math.log(4.0) - 2.0794415 * jax.random.uniform(key_list[4], (PLIES, ROWS, COLS), jnp.float32) ** shard_levels(key_list[4], (PLIES, ROWS, COLS), ((0, 8), (2, 64)), -0.2, 0.2)), 0.5, 4.0),
    }


relaxation = 2.0 / 3.0
half_root = 0.7071067811865476
fibre_modulus = 1.0
trans_modulus = 0.5
shear_modulus = 0.3
linear_fibre = 0.3
linear_trans = 0.8
square_fibre = 0.5
square_trans = 1.0
square_shear = 0.8
cross_term = -0.35


def ply_tables(angles):
    one_hot = (angles[:, None] == jnp.arange(4, dtype=jnp.int32)[None, :]).astype(jnp.float32)
    ply_cosine = jnp.sum(one_hot * jnp.array([1.0, half_root, half_root, 0.0], jnp.float32)[None, :], axis=1)
    ply_sine = jnp.sum(one_hot * jnp.array([0.0, half_root, -half_root, 1.0], jnp.float32)[None, :], axis=1)
    ply_cosine = ply_cosine.reshape(-1, 1, 1)
    ply_sine = ply_sine.reshape(-1, 1, 1)
    cond_rows = 4.0 * ply_cosine * ply_cosine + ply_sine * ply_sine
    cond_cols = 4.0 * ply_sine * ply_sine + ply_cosine * ply_cosine
    cond_cross = 3.0 * ply_cosine * ply_sine
    return cond_rows, cond_cols, cond_cross, ply_cosine, ply_sine


def tsai_wu(strain_x, strain_y, strain_xy, ply_cosine, ply_sine):
    cos_sq = ply_cosine * ply_cosine
    sin_sq = ply_sine * ply_sine
    mixed = ply_cosine * ply_sine
    fibre_strain = cos_sq * strain_x + sin_sq * strain_y + mixed * strain_xy
    trans_strain = sin_sq * strain_x + cos_sq * strain_y - mixed * strain_xy
    shear_strain = 2.0 * mixed * (strain_y - strain_x) + (cos_sq - sin_sq) * strain_xy
    fibre_stress = fibre_modulus * fibre_strain
    trans_stress = trans_modulus * trans_strain
    shear_stress = shear_modulus * shear_strain
    first = linear_fibre + 2.0 * square_fibre * fibre_stress + 2.0 * cross_term * trans_stress
    second = linear_trans + 2.0 * square_trans * trans_stress + 2.0 * cross_term * fibre_stress
    return first + second + 2.0 * square_shear * shear_stress


def sweep(padded, source, stiffening, coupling_up, coupling_down, cond_rows, cond_cols, cond_cross):
    widths = [(0, 0)] * (padded.ndim - 2) + [(1, 1), (0, 0)]
    framed = jnp.pad(padded, widths)
    centre = framed[..., 1:-1, 1:-1, 1:-1]
    along_rows = framed[..., 1:-1, 2:, 1:-1] + framed[..., 1:-1, :-2, 1:-1]
    along_cols = framed[..., 1:-1, 1:-1, 2:] + framed[..., 1:-1, 1:-1, :-2]
    diagonal_pairs = framed[..., 1:-1, 2:, 2:] + framed[..., 1:-1, :-2, :-2] - framed[..., 1:-1, 2:, :-2] - framed[..., 1:-1, :-2, 2:]
    overhead = framed[..., 2:, 1:-1, 1:-1]
    beneath = framed[..., :-2, 1:-1, 1:-1]
    image = cond_rows * (2.0 * centre - along_rows) + cond_cols * (2.0 * centre - along_cols) - 0.5 * cond_cross * diagonal_pairs
    image = image + coupling_up * (centre - overhead) + coupling_down * (centre - beneath) + stiffening * centre
    diagonal_sum = 2.0 * cond_rows + 2.0 * cond_cols + coupling_up + coupling_down + stiffening
    return centre + relaxation * (source - image) / diagonal_sum


def reference(strain, case_ids, angle_ids, stiffening, interface):
    cond_rows, cond_cols, cond_cross, ply_cosine, ply_sine = ply_tables(angle_ids)
    coupling_down = jnp.concatenate([jnp.zeros_like(interface[:1]), interface[:-1]], axis=0)

    def step_case(summed, case_id):
        components = lax.dynamic_index_in_dim(strain, case_id, 0, keepdims=False)
        source = tsai_wu(components[0], components[1], components[2], ply_cosine, ply_sine)
        adjoint = jnp.zeros(source.shape, jnp.float32)
        for iteration in range(ITERS):
            padded = jnp.pad(adjoint, ((1, 1), (0, 0), (1, 1)))
            adjoint = sweep(padded, source, stiffening, interface, coupling_down, cond_rows, cond_cols, cond_cross)
        return summed + adjoint * source, adjoint

    start = jnp.zeros(interface.shape, jnp.float32)
    summed, adjoint_all = lax.scan(step_case, start, case_ids)
    through = jnp.cumsum(summed, axis=0) / PLIES
    return adjoint_all, through
```

```python
import jax
import jax.numpy as jnp
from jax import lax
from jax.sharding import PartitionSpec as P

ITERS = 4


relaxation = 2.0 / 3.0
half_root = 0.7071067811865476
fibre_modulus = 1.0
trans_modulus = 0.5
shear_modulus = 0.3
linear_fibre = 0.3
linear_trans = 0.8
square_fibre = 0.5
square_trans = 1.0
square_shear = 0.8
cross_term = -0.35


def passed_along(array, axis, by):
    count = lax.axis_size(axis)
    pairs = [(i, i + by) for i in range(count) if 0 <= i + by < count]
    return lax.ppermute(array, axis, pairs)


def with_halos(block, axis, dim, below, above):
    size = block.shape[dim]
    low = passed_along(lax.slice_in_dim(block, size - below, size, axis=dim), axis, 1)
    high = passed_along(lax.slice_in_dim(block, 0, above, axis=dim), axis, -1)
    return jnp.concatenate([low, block, high], axis=dim)


def ply_tables(angles):
    one_hot = (angles[:, None] == jnp.arange(4, dtype=jnp.int32)[None, :]).astype(jnp.float32)
    ply_cosine = jnp.sum(
        one_hot * jnp.array([1.0, half_root, half_root, 0.0], jnp.float32)[None, :], axis=1
    )
    ply_sine = jnp.sum(
        one_hot * jnp.array([0.0, half_root, -half_root, 1.0], jnp.float32)[None, :], axis=1
    )
    ply_cosine = ply_cosine.reshape(-1, 1, 1)
    ply_sine = ply_sine.reshape(-1, 1, 1)
    cond_rows = 4.0 * ply_cosine * ply_cosine + ply_sine * ply_sine
    cond_cols = 4.0 * ply_sine * ply_sine + ply_cosine * ply_cosine
    cond_cross = 3.0 * ply_cosine * ply_sine
    return (cond_rows, cond_cols, cond_cross, ply_cosine, ply_sine)


def tsai_wu(strain_x, strain_y, strain_xy, ply_cosine, ply_sine):
    cos_sq = ply_cosine * ply_cosine
    sin_sq = ply_sine * ply_sine
    mixed = ply_cosine * ply_sine
    fibre_strain = cos_sq * strain_x + sin_sq * strain_y + mixed * strain_xy
    trans_strain = sin_sq * strain_x + cos_sq * strain_y - mixed * strain_xy
    shear_strain = 2.0 * mixed * (strain_y - strain_x) + (cos_sq - sin_sq) * strain_xy
    fibre_stress = fibre_modulus * fibre_strain
    trans_stress = trans_modulus * trans_strain
    shear_stress = shear_modulus * shear_strain
    first = linear_fibre + 2.0 * square_fibre * fibre_stress + 2.0 * cross_term * trans_stress
    second = linear_trans + 2.0 * square_trans * trans_stress + 2.0 * cross_term * fibre_stress
    return first + second + 2.0 * square_shear * shear_stress


def sweep(padded, source, stiffening, coupling_up, coupling_down, cond_rows, cond_cols, cond_cross):
    widths = [(0, 0)] * (padded.ndim - 2) + [(1, 1), (0, 0)]
    framed = jnp.pad(padded, widths)
    centre = framed[..., 1:-1, 1:-1, 1:-1]
    along_rows = framed[..., 1:-1, 2:, 1:-1] + framed[..., 1:-1, :-2, 1:-1]
    along_cols = framed[..., 1:-1, 1:-1, 2:] + framed[..., 1:-1, 1:-1, :-2]
    diagonal_pairs = (
        framed[..., 1:-1, 2:, 2:]
        + framed[..., 1:-1, :-2, :-2]
        - framed[..., 1:-1, 2:, :-2]
        - framed[..., 1:-1, :-2, 2:]
    )
    overhead = framed[..., 2:, 1:-1, 1:-1]
    beneath = framed[..., :-2, 1:-1, 1:-1]
    image = (
        cond_rows * (2.0 * centre - along_rows)
        + cond_cols * (2.0 * centre - along_cols)
        - 0.5 * cond_cross * diagonal_pairs
    )
    image = (
        image
        + coupling_up * (centre - overhead)
        + coupling_down * (centre - beneath)
        + stiffening * centre
    )
    diagonal_sum = 2.0 * cond_rows + 2.0 * cond_cols + coupling_up + coupling_down + stiffening
    return centre + relaxation * (source - image) / diagonal_sum


def trim(array, by, ply_dim, col_dim):
    if by == 0:
        return array
    array = lax.slice_in_dim(array, by, array.shape[ply_dim] - by, axis=ply_dim)
    return lax.slice_in_dim(array, by, array.shape[col_dim] - by, axis=col_dim)


def body(strain, case_ids, angle_ids, stiffening, interface):
    halo = ITERS - 1
    ply_local = angle_ids.shape[0]
    col_local = stiffening.shape[2]
    ply_count = lax.axis_size("ply")
    tile_count = lax.axis_size("tile")
    cases = case_ids.shape[0]
    chosen = jnp.take(strain, case_ids, axis=0)
    rows = chosen.shape[2]

    packed = jnp.concatenate(
        [chosen.reshape(cases * 3, rows, col_local), stiffening, interface], axis=0
    )
    packed = with_halos(packed, "tile", 2, halo, halo)
    width = col_local + 2 * halo
    strain_e = packed[: cases * 3].reshape(cases, 3, rows, width)
    stiff_c = packed[cases * 3 : cases * 3 + ply_local]
    inter_c = packed[cases * 3 + ply_local :]
    below = passed_along(
        jnp.concatenate([stiff_c[ply_local - halo :], inter_c[ply_local - halo - 1 :]], axis=0),
        "ply",
        1,
    )
    above = passed_along(jnp.concatenate([stiff_c[:halo], inter_c[:halo]], axis=0), "ply", -1)
    angles = with_halos(angle_ids, "ply", 0, halo, halo)
    stiff_e = jnp.concatenate([below[:halo], stiff_c, above[:halo]], axis=0)
    inter_all = jnp.concatenate([below[halo:], inter_c, above[halo:]], axis=0)
    up_e = inter_all[1:]
    down_e = inter_all[:-1]

    cond_rows, cond_cols, cond_cross, ply_cosine, ply_sine = ply_tables(angles)
    source_e = tsai_wu(
        strain_e[:, 0][:, None],
        strain_e[:, 1][:, None],
        strain_e[:, 2][:, None],
        ply_cosine,
        ply_sine,
    )
    ply_at = lax.axis_index("ply") * ply_local - halo + jnp.arange(ply_local + 2 * halo)
    col_at = lax.axis_index("tile") * col_local - halo + jnp.arange(width)
    inside = (
        ((ply_at >= 0) & (ply_at < ply_local * ply_count))[:, None, None]
        & ((col_at >= 0) & (col_at < col_local * tile_count))[None, None, :]
    ).astype(jnp.float32)

    diagonal_sum = 2.0 * cond_rows + 2.0 * cond_cols + up_e + down_e + stiff_e
    adjoint = relaxation * source_e / diagonal_sum * inside
    for iteration in range(1, ITERS):
        by = iteration
        adjoint = sweep(
            adjoint,
            trim(source_e, by, 1, 3),
            trim(stiff_e, by, 0, 2),
            trim(up_e, by, 0, 2),
            trim(down_e, by, 0, 2),
            cond_rows[by : cond_rows.shape[0] - by],
            cond_cols[by : cond_cols.shape[0] - by],
            cond_cross[by : cond_cross.shape[0] - by],
        )
        if iteration < ITERS - 1:
            adjoint = adjoint * trim(inside, by, 0, 2)
    source = trim(source_e, halo, 1, 3)
    summed = jnp.sum(adjoint * source, axis=0)
    running = jnp.cumsum(summed, axis=0)
    inclusive = running[-1]
    prefix = jnp.zeros_like(inclusive)
    shift = 1
    while shift < ply_count:
        arrived = passed_along(inclusive, "ply", shift)
        prefix = prefix + arrived
        inclusive = inclusive + arrived
        shift *= 2
    through = (running + prefix[None]) / (ply_local * ply_count)
    return (adjoint, through)


def solution(mesh):
    return jax.shard_map(
        body,
        mesh=mesh,
        in_specs=(
            P(None, None, None, "tile"),
            P(),
            P("ply"),
            P("ply", None, "tile"),
            P("ply", None, "tile"),
        ),
        out_specs=(P(None, "ply", None, "tile"), P("ply", None, "tile")),
        check_vma=False,
    )
```

```python
import jax
import jax.numpy as jnp
from jax import lax
from jax.sharding import PartitionSpec as P

ITERS = 4


relaxation = 2.0 / 3.0
half_root = 0.7071067811865476
fibre_modulus = 1.0
trans_modulus = 0.5
shear_modulus = 0.3
linear_fibre = 0.3
linear_trans = 0.8
square_fibre = 0.5
square_trans = 1.0
square_shear = 0.8
cross_term = -0.35


def passed_along(array, axis, by):
    count = lax.axis_size(axis)
    pairs = [(i, i + by) for i in range(count) if 0 <= i + by < count]
    return lax.ppermute(array, axis, pairs)


def with_halos(block, axis, dim, below, above):
    size = block.shape[dim]
    low = passed_along(lax.slice_in_dim(block, size - below, size, axis=dim), axis, 1)
    high = passed_along(lax.slice_in_dim(block, 0, above, axis=dim), axis, -1)
    return jnp.concatenate([low, block, high], axis=dim)


def ply_tables(angles):
    one_hot = (angles[:, None] == jnp.arange(4, dtype=jnp.int32)[None, :]).astype(jnp.float32)
    ply_cosine = jnp.sum(
        one_hot * jnp.array([1.0, half_root, half_root, 0.0], jnp.float32)[None, :], axis=1
    )
    ply_sine = jnp.sum(
        one_hot * jnp.array([0.0, half_root, -half_root, 1.0], jnp.float32)[None, :], axis=1
    )
    ply_cosine = ply_cosine.reshape(-1, 1, 1)
    ply_sine = ply_sine.reshape(-1, 1, 1)
    cond_rows = 4.0 * ply_cosine * ply_cosine + ply_sine * ply_sine
    cond_cols = 4.0 * ply_sine * ply_sine + ply_cosine * ply_cosine
    cond_cross = 3.0 * ply_cosine * ply_sine
    return (cond_rows, cond_cols, cond_cross, ply_cosine, ply_sine)


def tsai_wu(strain_x, strain_y, strain_xy, ply_cosine, ply_sine):
    cos_sq = ply_cosine * ply_cosine
    sin_sq = ply_sine * ply_sine
    mixed = ply_cosine * ply_sine
    fibre_strain = cos_sq * strain_x + sin_sq * strain_y + mixed * strain_xy
    trans_strain = sin_sq * strain_x + cos_sq * strain_y - mixed * strain_xy
    shear_strain = 2.0 * mixed * (strain_y - strain_x) + (cos_sq - sin_sq) * strain_xy
    fibre_stress = fibre_modulus * fibre_strain
    trans_stress = trans_modulus * trans_strain
    shear_stress = shear_modulus * shear_strain
    first = linear_fibre + 2.0 * square_fibre * fibre_stress + 2.0 * cross_term * trans_stress
    second = linear_trans + 2.0 * square_trans * trans_stress + 2.0 * cross_term * fibre_stress
    return first + second + 2.0 * square_shear * shear_stress


def sweep(padded, source, stiffening, coupling_up, coupling_down, cond_rows, cond_cols, cond_cross):
    widths = [(0, 0)] * (padded.ndim - 2) + [(1, 1), (0, 0)]
    framed = jnp.pad(padded, widths)
    centre = framed[..., 1:-1, 1:-1, 1:-1]
    along_rows = framed[..., 1:-1, 2:, 1:-1] + framed[..., 1:-1, :-2, 1:-1]
    along_cols = framed[..., 1:-1, 1:-1, 2:] + framed[..., 1:-1, 1:-1, :-2]
    diagonal_pairs = (
        framed[..., 1:-1, 2:, 2:]
        + framed[..., 1:-1, :-2, :-2]
        - framed[..., 1:-1, 2:, :-2]
        - framed[..., 1:-1, :-2, 2:]
    )
    overhead = framed[..., 2:, 1:-1, 1:-1]
    beneath = framed[..., :-2, 1:-1, 1:-1]
    image = (
        cond_rows * (2.0 * centre - along_rows)
        + cond_cols * (2.0 * centre - along_cols)
        - 0.5 * cond_cross * diagonal_pairs
    )
    image = (
        image
        + coupling_up * (centre - overhead)
        + coupling_down * (centre - beneath)
        + stiffening * centre
    )
    diagonal_sum = 2.0 * cond_rows + 2.0 * cond_cols + coupling_up + coupling_down + stiffening
    return centre + relaxation * (source - image) / diagonal_sum


def trim(array, by, ply_dim, col_dim):
    if by == 0:
        return array
    array = lax.slice_in_dim(array, by, array.shape[ply_dim] - by, axis=ply_dim)
    return lax.slice_in_dim(array, by, array.shape[col_dim] - by, axis=col_dim)


def passed_across(array, by_ply, by_tile):
    plies, tiles = lax.axis_size("ply"), lax.axis_size("tile")
    pairs = [
        (p * tiles + t, (p + by_ply) * tiles + t + by_tile)
        for p in range(plies)
        for t in range(tiles)
        if 0 <= p + by_ply < plies and 0 <= t + by_tile < tiles
    ]
    return lax.ppermute(array, ("ply", "tile"), pairs)


def body(strain, case_ids, angle_ids, stiffening, interface):
    halo = ITERS - 1
    ply_local = angle_ids.shape[0]
    col_local = stiffening.shape[2]
    ply_count = lax.axis_size("ply")
    tile_count = lax.axis_size("tile")
    cases = case_ids.shape[0]
    chosen = jnp.take(strain, case_ids, axis=0)
    rows = chosen.shape[2]
    width = col_local + 2 * halo

    flat = jnp.concatenate(
        [chosen.reshape(cases * 3, rows, col_local), stiffening, interface], axis=0
    )
    left = passed_along(flat[..., col_local - halo :], "tile", 1)
    right = passed_along(flat[..., :halo], "tile", -1)
    angle_plane = jnp.zeros((1, rows, col_local), jnp.float32)
    top_planes = jnp.concatenate(
        [stiffening[ply_local - halo :], interface[ply_local - halo - 1 :]], axis=0
    )
    bottom_planes = jnp.concatenate([stiffening[:halo], interface[:halo]], axis=0)
    below = passed_along(
        jnp.concatenate(
            [top_planes, angle_plane.at[0, 0, :halo].set(angle_ids[ply_local - halo :].astype(jnp.float32))],
            axis=0,
        ),
        "ply",
        1,
    )
    above = passed_along(
        jnp.concatenate(
            [bottom_planes, angle_plane.at[0, 0, :halo].set(angle_ids[:halo].astype(jnp.float32))],
            axis=0,
        ),
        "ply",
        -1,
    )
    below_left = passed_across(top_planes[..., col_local - halo :], 1, 1)
    below_right = passed_across(top_planes[..., :halo], 1, -1)
    above_left = passed_across(bottom_planes[..., col_local - halo :], -1, 1)
    above_right = passed_across(bottom_planes[..., :halo], -1, -1)

    packed = jnp.concatenate([left, flat, right], axis=2)
    strain_e = packed[: cases * 3].reshape(cases, 3, rows, width)
    stiff_c = packed[cases * 3 : cases * 3 + ply_local]
    inter_c = packed[cases * 3 + ply_local :]
    below_e = jnp.concatenate([below_left, below[: 2 * halo + 1], below_right], axis=2)
    above_e = jnp.concatenate([above_left, above[: 2 * halo], above_right], axis=2)
    stiff_e = jnp.concatenate([below_e[:halo], stiff_c, above_e[:halo]], axis=0)
    inter_all = jnp.concatenate([below_e[halo:], inter_c, above_e[halo:]], axis=0)
    up_e = inter_all[1:]
    down_e = inter_all[:-1]
    angles = jnp.concatenate(
        [
            below[2 * halo + 1, 0, :halo].astype(jnp.int32),
            angle_ids,
            above[2 * halo, 0, :halo].astype(jnp.int32),
        ]
    )

    cond_rows, cond_cols, cond_cross, ply_cosine, ply_sine = ply_tables(angles)
    source_e = tsai_wu(
        strain_e[:, 0][:, None],
        strain_e[:, 1][:, None],
        strain_e[:, 2][:, None],
        ply_cosine,
        ply_sine,
    )
    ply_at = lax.axis_index("ply") * ply_local - halo + jnp.arange(ply_local + 2 * halo)
    col_at = lax.axis_index("tile") * col_local - halo + jnp.arange(width)
    inside = (
        ((ply_at >= 0) & (ply_at < ply_local * ply_count))[:, None, None]
        & ((col_at >= 0) & (col_at < col_local * tile_count))[None, None, :]
    ).astype(jnp.float32)

    diagonal_sum = 2.0 * cond_rows + 2.0 * cond_cols + up_e + down_e + stiff_e
    adjoint = relaxation * source_e / diagonal_sum * inside
    for iteration in range(1, ITERS):
        by = iteration
        adjoint = sweep(
            adjoint,
            trim(source_e, by, 1, 3),
            trim(stiff_e, by, 0, 2),
            trim(up_e, by, 0, 2),
            trim(down_e, by, 0, 2),
            cond_rows[by : cond_rows.shape[0] - by],
            cond_cols[by : cond_cols.shape[0] - by],
            cond_cross[by : cond_cross.shape[0] - by],
        )
        if iteration < ITERS - 1:
            adjoint = adjoint * trim(inside, by, 0, 2)
    source = trim(source_e, halo, 1, 3)
    product = adjoint * source
    total = jnp.sum(product, axis=(0, 1))
    arrivals = [passed_along(total, "ply", shift) for shift in range(1, ply_count)]
    running = jnp.cumsum(jnp.sum(product, axis=0), axis=0)
    prefix = arrivals[0]
    for arrived in arrivals[1:]:
        prefix = prefix + arrived
    through = (running + prefix[None]) / (ply_local * ply_count)
    return (adjoint, through)


def solution(mesh):
    return jax.shard_map(
        body,
        mesh=mesh,
        in_specs=(
            P(None, None, None, "tile"),
            P(),
            P("ply"),
            P("ply", None, "tile"),
            P("ply", None, "tile"),
        ),
        out_specs=(P(None, "ply", None, "tile"), P("ply", None, "tile")),
        check_vma=False,
    )
```

```python
import jax
import jax.numpy as jnp
from jax import lax
from jax.sharding import PartitionSpec as P

ITERS = 4


relaxation = 2.0 / 3.0
half_root = 0.7071067811865476
fibre_modulus = 1.0
trans_modulus = 0.5
shear_modulus = 0.3
linear_fibre = 0.3
linear_trans = 0.8
square_fibre = 0.5
square_trans = 1.0
square_shear = 0.8
cross_term = -0.35


def passed_along(array, axis, by):
    count = lax.axis_size(axis)
    pairs = [(i, i + by) for i in range(count) if 0 <= i + by < count]
    return lax.ppermute(array, axis, pairs)


def with_halos(block, axis, dim, below, above):
    size = block.shape[dim]
    low = passed_along(lax.slice_in_dim(block, size - below, size, axis=dim), axis, 1)
    high = passed_along(lax.slice_in_dim(block, 0, above, axis=dim), axis, -1)
    return jnp.concatenate([low, block, high], axis=dim)


def ply_tables(angles):
    one_hot = (angles[:, None] == jnp.arange(4, dtype=jnp.int32)[None, :]).astype(jnp.float32)
    ply_cosine = jnp.sum(
        one_hot * jnp.array([1.0, half_root, half_root, 0.0], jnp.float32)[None, :], axis=1
    )
    ply_sine = jnp.sum(
        one_hot * jnp.array([0.0, half_root, -half_root, 1.0], jnp.float32)[None, :], axis=1
    )
    ply_cosine = ply_cosine.reshape(-1, 1, 1)
    ply_sine = ply_sine.reshape(-1, 1, 1)
    cond_rows = 4.0 * ply_cosine * ply_cosine + ply_sine * ply_sine
    cond_cols = 4.0 * ply_sine * ply_sine + ply_cosine * ply_cosine
    cond_cross = 3.0 * ply_cosine * ply_sine
    return (cond_rows, cond_cols, cond_cross, ply_cosine, ply_sine)


def tsai_wu(strain_x, strain_y, strain_xy, ply_cosine, ply_sine):
    cos_sq = ply_cosine * ply_cosine
    sin_sq = ply_sine * ply_sine
    mixed = ply_cosine * ply_sine
    fibre_strain = cos_sq * strain_x + sin_sq * strain_y + mixed * strain_xy
    trans_strain = sin_sq * strain_x + cos_sq * strain_y - mixed * strain_xy
    shear_strain = 2.0 * mixed * (strain_y - strain_x) + (cos_sq - sin_sq) * strain_xy
    fibre_stress = fibre_modulus * fibre_strain
    trans_stress = trans_modulus * trans_strain
    shear_stress = shear_modulus * shear_strain
    first = linear_fibre + 2.0 * square_fibre * fibre_stress + 2.0 * cross_term * trans_stress
    second = linear_trans + 2.0 * square_trans * trans_stress + 2.0 * cross_term * fibre_stress
    return first + second + 2.0 * square_shear * shear_stress


def sweep(padded, source, stiffening, coupling_up, coupling_down, cond_rows, cond_cols, cond_cross):
    widths = [(0, 0)] * (padded.ndim - 2) + [(1, 1), (0, 0)]
    framed = jnp.pad(padded, widths)
    centre = framed[..., 1:-1, 1:-1, 1:-1]
    along_rows = framed[..., 1:-1, 2:, 1:-1] + framed[..., 1:-1, :-2, 1:-1]
    along_cols = framed[..., 1:-1, 1:-1, 2:] + framed[..., 1:-1, 1:-1, :-2]
    diagonal_pairs = (
        framed[..., 1:-1, 2:, 2:]
        + framed[..., 1:-1, :-2, :-2]
        - framed[..., 1:-1, 2:, :-2]
        - framed[..., 1:-1, :-2, 2:]
    )
    overhead = framed[..., 2:, 1:-1, 1:-1]
    beneath = framed[..., :-2, 1:-1, 1:-1]
    image = (
        cond_rows * (2.0 * centre - along_rows)
        + cond_cols * (2.0 * centre - along_cols)
        - 0.5 * cond_cross * diagonal_pairs
    )
    image = (
        image
        + coupling_up * (centre - overhead)
        + coupling_down * (centre - beneath)
        + stiffening * centre
    )
    diagonal_sum = 2.0 * cond_rows + 2.0 * cond_cols + coupling_up + coupling_down + stiffening
    return centre + relaxation * (source - image) / diagonal_sum


def trim(array, by, ply_dim, col_dim):
    if by == 0:
        return array
    array = lax.slice_in_dim(array, by, array.shape[ply_dim] - by, axis=ply_dim)
    return lax.slice_in_dim(array, by, array.shape[col_dim] - by, axis=col_dim)


def body(strain, case_ids, angle_ids, stiffening, interface):
    halo = ITERS - 1
    ply_local = angle_ids.shape[0]
    col_local = stiffening.shape[2]
    ply_count = lax.axis_size("ply")
    tile_count = lax.axis_size("tile")
    cases = case_ids.shape[0]
    chosen = jnp.take(strain, case_ids, axis=0)
    rows = chosen.shape[2]

    packed = jnp.concatenate(
        [chosen.reshape(cases * 3, rows, col_local), stiffening, interface], axis=0
    )
    packed = with_halos(packed, "tile", 2, halo, halo)
    width = col_local + 2 * halo
    strain_e = packed[: cases * 3].reshape(cases, 3, rows, width)
    stiff_c = packed[cases * 3 : cases * 3 + ply_local]
    inter_c = packed[cases * 3 + ply_local :]
    below = passed_along(
        jnp.concatenate([stiff_c[ply_local - halo :], inter_c[ply_local - halo - 1 :]], axis=0),
        "ply",
        1,
    )
    above = passed_along(jnp.concatenate([stiff_c[:halo], inter_c[:halo]], axis=0), "ply", -1)
    angles = with_halos(angle_ids, "ply", 0, halo, halo)
    stiff_e = jnp.concatenate([below[:halo], stiff_c, above[:halo]], axis=0)
    inter_all = jnp.concatenate([below[halo:], inter_c, above[halo:]], axis=0)
    up_e = inter_all[1:]
    down_e = inter_all[:-1]

    cond_rows, cond_cols, cond_cross, ply_cosine, ply_sine = ply_tables(angles)
    source_e = tsai_wu(
        strain_e[:, 0][:, None],
        strain_e[:, 1][:, None],
        strain_e[:, 2][:, None],
        ply_cosine,
        ply_sine,
    )
    ply_at = lax.axis_index("ply") * ply_local - halo + jnp.arange(ply_local + 2 * halo)
    col_at = lax.axis_index("tile") * col_local - halo + jnp.arange(width)
    inside = (
        ((ply_at >= 0) & (ply_at < ply_local * ply_count))[:, None, None]
        & ((col_at >= 0) & (col_at < col_local * tile_count))[None, None, :]
    ).astype(jnp.float32)

    diagonal_sum = 2.0 * cond_rows + 2.0 * cond_cols + up_e + down_e + stiff_e
    adjoint = relaxation * source_e / diagonal_sum * inside
    for iteration in range(1, ITERS):
        by = iteration
        adjoint = sweep(
            adjoint,
            trim(source_e, by, 1, 3),
            trim(stiff_e, by, 0, 2),
            trim(up_e, by, 0, 2),
            trim(down_e, by, 0, 2),
            cond_rows[by : cond_rows.shape[0] - by],
            cond_cols[by : cond_cols.shape[0] - by],
            cond_cross[by : cond_cross.shape[0] - by],
        )
        if iteration < ITERS - 1:
            adjoint = adjoint * trim(inside, by, 0, 2)
    source = trim(source_e, halo, 1, 3)
    product = adjoint * source
    total = jnp.sum(product, axis=(0, 1))
    arrivals = [passed_along(total, "ply", shift) for shift in range(1, ply_count)]
    running = jnp.cumsum(jnp.sum(product, axis=0), axis=0)
    prefix = arrivals[0]
    for arrived in arrivals[1:]:
        prefix = prefix + arrived
    through = (running + prefix[None]) / (ply_local * ply_count)
    return (adjoint, through)


def solution(mesh):
    return jax.shard_map(
        body,
        mesh=mesh,
        in_specs=(
            P(None, None, None, "tile"),
            P(),
            P("ply"),
            P("ply", None, "tile"),
            P("ply", None, "tile"),
        ),
        out_specs=(P(None, "ply", None, "tile"), P("ply", None, "tile")),
        check_vma=False,
    )
```

```python
import jax
import jax.numpy as jnp
from jax import lax
from jax.sharding import PartitionSpec as P

ITERS = 4


relaxation = 2.0 / 3.0
half_root = 0.7071067811865476
fibre_modulus = 1.0
trans_modulus = 0.5
shear_modulus = 0.3
linear_fibre = 0.3
linear_trans = 0.8
square_fibre = 0.5
square_trans = 1.0
square_shear = 0.8
cross_term = -0.35


def passed_along(array, axis, by):
    count = lax.axis_size(axis)
    pairs = [(i, i + by) for i in range(count) if 0 <= i + by < count]
    return lax.ppermute(array, axis, pairs)


def with_halos(block, axis, dim, below, above):
    size = block.shape[dim]
    low = passed_along(lax.slice_in_dim(block, size - below, size, axis=dim), axis, 1)
    high = passed_along(lax.slice_in_dim(block, 0, above, axis=dim), axis, -1)
    return jnp.concatenate([low, block, high], axis=dim)


def ply_tables(angles):
    one_hot = (angles[:, None] == jnp.arange(4, dtype=jnp.int32)[None, :]).astype(jnp.float32)
    ply_cosine = jnp.sum(
        one_hot * jnp.array([1.0, half_root, half_root, 0.0], jnp.float32)[None, :], axis=1
    )
    ply_sine = jnp.sum(
        one_hot * jnp.array([0.0, half_root, -half_root, 1.0], jnp.float32)[None, :], axis=1
    )
    ply_cosine = ply_cosine.reshape(-1, 1, 1)
    ply_sine = ply_sine.reshape(-1, 1, 1)
    cond_rows = 4.0 * ply_cosine * ply_cosine + ply_sine * ply_sine
    cond_cols = 4.0 * ply_sine * ply_sine + ply_cosine * ply_cosine
    cond_cross = 3.0 * ply_cosine * ply_sine
    return (cond_rows, cond_cols, cond_cross, ply_cosine, ply_sine)


def tsai_wu(strain_x, strain_y, strain_xy, ply_cosine, ply_sine):
    cos_sq = ply_cosine * ply_cosine
    sin_sq = ply_sine * ply_sine
    mixed = ply_cosine * ply_sine
    fibre_strain = cos_sq * strain_x + sin_sq * strain_y + mixed * strain_xy
    trans_strain = sin_sq * strain_x + cos_sq * strain_y - mixed * strain_xy
    shear_strain = 2.0 * mixed * (strain_y - strain_x) + (cos_sq - sin_sq) * strain_xy
    fibre_stress = fibre_modulus * fibre_strain
    trans_stress = trans_modulus * trans_strain
    shear_stress = shear_modulus * shear_strain
    first = linear_fibre + 2.0 * square_fibre * fibre_stress + 2.0 * cross_term * trans_stress
    second = linear_trans + 2.0 * square_trans * trans_stress + 2.0 * cross_term * fibre_stress
    return first + second + 2.0 * square_shear * shear_stress


def sweep(padded, source, stiffening, coupling_up, coupling_down, cond_rows, cond_cols, cond_cross, scale):
    widths = [(0, 0)] * (padded.ndim - 2) + [(1, 1), (0, 0)]
    framed = jnp.pad(padded, widths)
    centre = framed[..., 1:-1, 1:-1, 1:-1]
    along_rows = framed[..., 1:-1, 2:, 1:-1] + framed[..., 1:-1, :-2, 1:-1]
    along_cols = framed[..., 1:-1, 1:-1, 2:] + framed[..., 1:-1, 1:-1, :-2]
    diagonal_pairs = (
        framed[..., 1:-1, 2:, 2:]
        + framed[..., 1:-1, :-2, :-2]
        - framed[..., 1:-1, 2:, :-2]
        - framed[..., 1:-1, :-2, 2:]
    )
    overhead = framed[..., 2:, 1:-1, 1:-1]
    beneath = framed[..., :-2, 1:-1, 1:-1]
    image = (
        cond_rows * (2.0 * centre - along_rows)
        + cond_cols * (2.0 * centre - along_cols)
        - 0.5 * cond_cross * diagonal_pairs
    )
    image = (
        image
        + coupling_up * (centre - overhead)
        + coupling_down * (centre - beneath)
        + stiffening * centre
    )
    return centre + (source - image) * scale


def trim(array, by, ply_dim, col_dim):
    if by == 0:
        return array
    array = lax.slice_in_dim(array, by, array.shape[ply_dim] - by, axis=ply_dim)
    return lax.slice_in_dim(array, by, array.shape[col_dim] - by, axis=col_dim)


def body(strain, case_ids, angle_ids, stiffening, interface):
    halo = ITERS - 1
    ply_local = angle_ids.shape[0]
    col_local = stiffening.shape[2]
    ply_count = lax.axis_size("ply")
    tile_count = lax.axis_size("tile")
    cases = case_ids.shape[0]
    chosen = jnp.take(strain, case_ids, axis=0)
    rows = chosen.shape[2]

    packed = jnp.concatenate(
        [chosen.reshape(cases * 3, rows, col_local), stiffening, interface], axis=0
    )
    packed = with_halos(packed, "tile", 2, halo, halo)
    width = col_local + 2 * halo
    strain_e = packed[: cases * 3].reshape(cases, 3, rows, width)
    stiff_c = packed[cases * 3 : cases * 3 + ply_local]
    inter_c = packed[cases * 3 + ply_local :]
    angle_plane = jnp.zeros((1, rows, width), jnp.float32)
    below = passed_along(
        jnp.concatenate(
            [
                stiff_c[ply_local - halo :],
                inter_c[ply_local - halo - 1 :],
                angle_plane.at[0, 0, :halo].set(angle_ids[ply_local - halo :].astype(jnp.float32)),
            ],
            axis=0,
        ),
        "ply",
        1,
    )
    above = passed_along(
        jnp.concatenate(
            [
                stiff_c[:halo],
                inter_c[:halo],
                angle_plane.at[0, 0, :halo].set(angle_ids[:halo].astype(jnp.float32)),
            ],
            axis=0,
        ),
        "ply",
        -1,
    )
    angles = jnp.concatenate(
        [
            below[2 * halo + 1, 0, :halo].astype(jnp.int32),
            angle_ids,
            above[2 * halo, 0, :halo].astype(jnp.int32),
        ]
    )
    below = below[: 2 * halo + 1]
    above = above[: 2 * halo]
    stiff_e = jnp.concatenate([below[:halo], stiff_c, above[:halo]], axis=0)
    inter_all = jnp.concatenate([below[halo:], inter_c, above[halo:]], axis=0)
    up_e = inter_all[1:]
    down_e = inter_all[:-1]

    cond_rows, cond_cols, cond_cross, ply_cosine, ply_sine = ply_tables(angles)
    source_e = tsai_wu(
        strain_e[:, 0][:, None],
        strain_e[:, 1][:, None],
        strain_e[:, 2][:, None],
        ply_cosine,
        ply_sine,
    )
    ply_at = lax.axis_index("ply") * ply_local - halo + jnp.arange(ply_local + 2 * halo)
    col_at = lax.axis_index("tile") * col_local - halo + jnp.arange(width)
    inside = (
        ((ply_at >= 0) & (ply_at < ply_local * ply_count))[:, None, None]
        & ((col_at >= 0) & (col_at < col_local * tile_count))[None, None, :]
    ).astype(jnp.float32)

    diagonal_sum = 2.0 * cond_rows + 2.0 * cond_cols + up_e + down_e + stiff_e
    scale_e = relaxation / diagonal_sum
    adjoint = source_e * scale_e * inside
    for iteration in range(1, ITERS):
        by = iteration
        adjoint = sweep(
            adjoint,
            trim(source_e, by, 1, 3),
            trim(stiff_e, by, 0, 2),
            trim(up_e, by, 0, 2),
            trim(down_e, by, 0, 2),
            cond_rows[by : cond_rows.shape[0] - by],
            cond_cols[by : cond_cols.shape[0] - by],
            cond_cross[by : cond_cross.shape[0] - by],
            trim(scale_e, by, 0, 2),
        )
        if iteration < ITERS - 1:
            adjoint = adjoint * trim(inside, by, 0, 2)
    source = trim(source_e, halo, 1, 3)
    product = adjoint * source
    total = jnp.sum(product, axis=(0, 1))
    totals = lax.all_to_all(
        jnp.broadcast_to(total[None], (ply_count,) + total.shape), "ply", 0, 0, tiled=True
    )
    lower = (jnp.arange(ply_count) < lax.axis_index("ply")).astype(jnp.float32)
    prefix = jnp.sum(totals * lower[:, None, None], axis=0)
    running = jnp.cumsum(jnp.sum(product, axis=0), axis=0)
    through = (running + prefix[None]) / (ply_local * ply_count)
    return (adjoint, through)


def solution(mesh):
    return jax.shard_map(
        body,
        mesh=mesh,
        in_specs=(
            P(None, None, None, "tile"),
            P(),
            P("ply"),
            P("ply", None, "tile"),
            P("ply", None, "tile"),
        ),
        out_specs=(P(None, "ply", None, "tile"), P("ply", None, "tile")),
        check_vma=False,
    )
```

```python
import jax
import jax.numpy as jnp
from jax import lax
from jax.sharding import PartitionSpec as P

ITERS = 4


relaxation = 2.0 / 3.0
half_root = 0.7071067811865476
fibre_modulus = 1.0
trans_modulus = 0.5
shear_modulus = 0.3
linear_fibre = 0.3
linear_trans = 0.8
square_fibre = 0.5
square_trans = 1.0
square_shear = 0.8
cross_term = -0.35


def passed_along(array, axis, by):
    count = lax.axis_size(axis)
    pairs = [(i, i + by) for i in range(count) if 0 <= i + by < count]
    return lax.ppermute(array, axis, pairs)


def with_halos(block, axis, dim, below, above):
    size = block.shape[dim]
    low = passed_along(lax.slice_in_dim(block, size - below, size, axis=dim), axis, 1)
    high = passed_along(lax.slice_in_dim(block, 0, above, axis=dim), axis, -1)
    return jnp.concatenate([low, block, high], axis=dim)


def ply_tables(angles):
    one_hot = (angles[:, None] == jnp.arange(4, dtype=jnp.int32)[None, :]).astype(jnp.float32)
    ply_cosine = jnp.sum(
        one_hot * jnp.array([1.0, half_root, half_root, 0.0], jnp.float32)[None, :], axis=1
    )
    ply_sine = jnp.sum(
        one_hot * jnp.array([0.0, half_root, -half_root, 1.0], jnp.float32)[None, :], axis=1
    )
    ply_cosine = ply_cosine.reshape(-1, 1, 1)
    ply_sine = ply_sine.reshape(-1, 1, 1)
    cond_rows = 4.0 * ply_cosine * ply_cosine + ply_sine * ply_sine
    cond_cols = 4.0 * ply_sine * ply_sine + ply_cosine * ply_cosine
    cond_cross = 3.0 * ply_cosine * ply_sine
    return (cond_rows, cond_cols, cond_cross, ply_cosine, ply_sine)


def tsai_wu(strain_x, strain_y, strain_xy, ply_cosine, ply_sine):
    cos_sq = ply_cosine * ply_cosine
    sin_sq = ply_sine * ply_sine
    mixed = ply_cosine * ply_sine
    fibre_strain = cos_sq * strain_x + sin_sq * strain_y + mixed * strain_xy
    trans_strain = sin_sq * strain_x + cos_sq * strain_y - mixed * strain_xy
    shear_strain = 2.0 * mixed * (strain_y - strain_x) + (cos_sq - sin_sq) * strain_xy
    fibre_stress = fibre_modulus * fibre_strain
    trans_stress = trans_modulus * trans_strain
    shear_stress = shear_modulus * shear_strain
    first = linear_fibre + 2.0 * square_fibre * fibre_stress + 2.0 * cross_term * trans_stress
    second = linear_trans + 2.0 * square_trans * trans_stress + 2.0 * cross_term * fibre_stress
    return first + second + 2.0 * square_shear * shear_stress


def sweep(padded, source, stiffening, coupling_up, coupling_down, cond_rows, cond_cols, cond_cross):
    widths = [(0, 0)] * (padded.ndim - 2) + [(1, 1), (0, 0)]
    framed = jnp.pad(padded, widths)
    centre = framed[..., 1:-1, 1:-1, 1:-1]
    along_rows = framed[..., 1:-1, 2:, 1:-1] + framed[..., 1:-1, :-2, 1:-1]
    along_cols = framed[..., 1:-1, 1:-1, 2:] + framed[..., 1:-1, 1:-1, :-2]
    diagonal_pairs = (
        framed[..., 1:-1, 2:, 2:]
        + framed[..., 1:-1, :-2, :-2]
        - framed[..., 1:-1, 2:, :-2]
        - framed[..., 1:-1, :-2, 2:]
    )
    overhead = framed[..., 2:, 1:-1, 1:-1]
    beneath = framed[..., :-2, 1:-1, 1:-1]
    image = (
        cond_rows * (2.0 * centre - along_rows)
        + cond_cols * (2.0 * centre - along_cols)
        - 0.5 * cond_cross * diagonal_pairs
    )
    image = (
        image
        + coupling_up * (centre - overhead)
        + coupling_down * (centre - beneath)
        + stiffening * centre
    )
    diagonal_sum = 2.0 * cond_rows + 2.0 * cond_cols + coupling_up + coupling_down + stiffening
    return centre + relaxation * (source - image) / diagonal_sum


def trim(array, by, ply_dim, col_dim):
    if by == 0:
        return array
    array = lax.slice_in_dim(array, by, array.shape[ply_dim] - by, axis=ply_dim)
    return lax.slice_in_dim(array, by, array.shape[col_dim] - by, axis=col_dim)


def body(strain, case_ids, angle_ids, stiffening, interface):
    halo = ITERS - 1
    ply_local = angle_ids.shape[0]
    col_local = stiffening.shape[2]
    ply_count = lax.axis_size("ply")
    tile_count = lax.axis_size("tile")
    cases = case_ids.shape[0]
    chosen = jnp.take(strain, case_ids, axis=0)
    rows = chosen.shape[2]

    packed = jnp.concatenate(
        [chosen.reshape(cases * 3, rows, col_local), stiffening, interface], axis=0
    )
    packed = with_halos(packed, "tile", 2, halo, halo)
    width = col_local + 2 * halo
    strain_e = packed[: cases * 3].reshape(cases, 3, rows, width)
    stiff_c = packed[cases * 3 : cases * 3 + ply_local]
    inter_c = packed[cases * 3 + ply_local :]
    angle_plane = jnp.zeros((1, rows, width), jnp.float32)
    below = passed_along(
        jnp.concatenate(
            [
                stiff_c[ply_local - halo :],
                inter_c[ply_local - halo - 1 :],
                angle_plane.at[0, 0, :halo].set(angle_ids[ply_local - halo :].astype(jnp.float32)),
            ],
            axis=0,
        ),
        "ply",
        1,
    )
    above = passed_along(
        jnp.concatenate(
            [
                stiff_c[:halo],
                inter_c[:halo],
                angle_plane.at[0, 0, :halo].set(angle_ids[:halo].astype(jnp.float32)),
            ],
            axis=0,
        ),
        "ply",
        -1,
    )
    angles = jnp.concatenate(
        [
            below[2 * halo + 1, 0, :halo].astype(jnp.int32),
            angle_ids,
            above[2 * halo, 0, :halo].astype(jnp.int32),
        ]
    )
    below = below[: 2 * halo + 1]
    above = above[: 2 * halo]
    stiff_e = jnp.concatenate([below[:halo], stiff_c, above[:halo]], axis=0)
    inter_all = jnp.concatenate([below[halo:], inter_c, above[halo:]], axis=0)
    up_e = inter_all[1:]
    down_e = inter_all[:-1]

    cond_rows, cond_cols, cond_cross, ply_cosine, ply_sine = ply_tables(angles)
    source_e = tsai_wu(
        strain_e[:, 0][:, None],
        strain_e[:, 1][:, None],
        strain_e[:, 2][:, None],
        ply_cosine,
        ply_sine,
    )
    ply_at = lax.axis_index("ply") * ply_local - halo + jnp.arange(ply_local + 2 * halo)
    col_at = lax.axis_index("tile") * col_local - halo + jnp.arange(width)
    inside = (
        ((ply_at >= 0) & (ply_at < ply_local * ply_count))[:, None, None]
        & ((col_at >= 0) & (col_at < col_local * tile_count))[None, None, :]
    ).astype(jnp.float32)

    diagonal_sum = 2.0 * cond_rows + 2.0 * cond_cols + up_e + down_e + stiff_e
    adjoint = relaxation * source_e / diagonal_sum * inside
    for iteration in range(1, ITERS):
        by = iteration
        adjoint = sweep(
            adjoint,
            trim(source_e, by, 1, 3),
            trim(stiff_e, by, 0, 2),
            trim(up_e, by, 0, 2),
            trim(down_e, by, 0, 2),
            cond_rows[by : cond_rows.shape[0] - by],
            cond_cols[by : cond_cols.shape[0] - by],
            cond_cross[by : cond_cross.shape[0] - by],
        )
        if iteration < ITERS - 1:
            adjoint = adjoint * trim(inside, by, 0, 2)
    source = trim(source_e, halo, 1, 3)
    product = adjoint * source
    total = jnp.sum(product, axis=(0, 1))
    totals = lax.all_to_all(
        jnp.broadcast_to(total[None], (ply_count,) + total.shape), "ply", 0, 0, tiled=True
    )
    lower = (jnp.arange(ply_count) < lax.axis_index("ply")).astype(jnp.float32)
    prefix = jnp.sum(totals * lower[:, None, None], axis=0)
    running = jnp.cumsum(jnp.sum(product, axis=0), axis=0)
    through = (running + prefix[None]) / (ply_local * ply_count)
    return (adjoint, through)


def solution(mesh):
    return jax.shard_map(
        body,
        mesh=mesh,
        in_specs=(
            P(None, None, None, "tile"),
            P(),
            P("ply"),
            P("ply", None, "tile"),
            P("ply", None, "tile"),
        ),
        out_specs=(P(None, "ply", None, "tile"), P("ply", None, "tile")),
        check_vma=False,
    )
```

```python
import jax
import jax.numpy as jnp
from jax import lax
from jax.sharding import PartitionSpec as P

ITERS = 4


relaxation = 2.0 / 3.0
half_root = 0.7071067811865476
fibre_modulus = 1.0
trans_modulus = 0.5
shear_modulus = 0.3
linear_fibre = 0.3
linear_trans = 0.8
square_fibre = 0.5
square_trans = 1.0
square_shear = 0.8
cross_term = -0.35


def passed_along(array, axis, by):
    count = lax.axis_size(axis)
    pairs = [(i, i + by) for i in range(count) if 0 <= i + by < count]
    return lax.ppermute(array, axis, pairs)


def with_halos(block, axis, dim, below, above):
    size = block.shape[dim]
    low = passed_along(lax.slice_in_dim(block, size - below, size, axis=dim), axis, 1)
    high = passed_along(lax.slice_in_dim(block, 0, above, axis=dim), axis, -1)
    return jnp.concatenate([low, block, high], axis=dim)


def ply_tables(angles):
    one_hot = (angles[:, None] == jnp.arange(4, dtype=jnp.int32)[None, :]).astype(jnp.float32)
    ply_cosine = jnp.sum(
        one_hot * jnp.array([1.0, half_root, half_root, 0.0], jnp.float32)[None, :], axis=1
    )
    ply_sine = jnp.sum(
        one_hot * jnp.array([0.0, half_root, -half_root, 1.0], jnp.float32)[None, :], axis=1
    )
    ply_cosine = ply_cosine.reshape(-1, 1, 1)
    ply_sine = ply_sine.reshape(-1, 1, 1)
    cond_rows = 4.0 * ply_cosine * ply_cosine + ply_sine * ply_sine
    cond_cols = 4.0 * ply_sine * ply_sine + ply_cosine * ply_cosine
    cond_cross = 3.0 * ply_cosine * ply_sine
    return (cond_rows, cond_cols, cond_cross, ply_cosine, ply_sine)


def tsai_wu(strain_x, strain_y, strain_xy, ply_cosine, ply_sine):
    cos_sq = ply_cosine * ply_cosine
    sin_sq = ply_sine * ply_sine
    mixed = ply_cosine * ply_sine
    fibre_strain = cos_sq * strain_x + sin_sq * strain_y + mixed * strain_xy
    trans_strain = sin_sq * strain_x + cos_sq * strain_y - mixed * strain_xy
    shear_strain = 2.0 * mixed * (strain_y - strain_x) + (cos_sq - sin_sq) * strain_xy
    fibre_stress = fibre_modulus * fibre_strain
    trans_stress = trans_modulus * trans_strain
    shear_stress = shear_modulus * shear_strain
    first = linear_fibre + 2.0 * square_fibre * fibre_stress + 2.0 * cross_term * trans_stress
    second = linear_trans + 2.0 * square_trans * trans_stress + 2.0 * cross_term * fibre_stress
    return first + second + 2.0 * square_shear * shear_stress


def sweep(padded, source, stiffening, coupling_up, coupling_down, cond_rows, cond_cols, cond_cross):
    widths = [(0, 0)] * (padded.ndim - 2) + [(1, 1), (0, 0)]
    framed = jnp.pad(padded, widths)
    centre = framed[..., 1:-1, 1:-1, 1:-1]
    along_rows = framed[..., 1:-1, 2:, 1:-1] + framed[..., 1:-1, :-2, 1:-1]
    along_cols = framed[..., 1:-1, 1:-1, 2:] + framed[..., 1:-1, 1:-1, :-2]
    diagonal_pairs = (
        framed[..., 1:-1, 2:, 2:]
        + framed[..., 1:-1, :-2, :-2]
        - framed[..., 1:-1, 2:, :-2]
        - framed[..., 1:-1, :-2, 2:]
    )
    overhead = framed[..., 2:, 1:-1, 1:-1]
    beneath = framed[..., :-2, 1:-1, 1:-1]
    image = (
        cond_rows * (2.0 * centre - along_rows)
        + cond_cols * (2.0 * centre - along_cols)
        - 0.5 * cond_cross * diagonal_pairs
    )
    image = (
        image
        + coupling_up * (centre - overhead)
        + coupling_down * (centre - beneath)
        + stiffening * centre
    )
    diagonal_sum = 2.0 * cond_rows + 2.0 * cond_cols + coupling_up + coupling_down + stiffening
    return centre + relaxation * (source - image) / diagonal_sum


def trim(array, by, ply_dim, col_dim):
    if by == 0:
        return array
    array = lax.slice_in_dim(array, by, array.shape[ply_dim] - by, axis=ply_dim)
    return lax.slice_in_dim(array, by, array.shape[col_dim] - by, axis=col_dim)


def body(strain, case_ids, angle_ids, stiffening, interface):
    halo = ITERS - 1
    ply_local = angle_ids.shape[0]
    col_local = stiffening.shape[2]
    ply_count = lax.axis_size("ply")
    tile_count = lax.axis_size("tile")
    cases = case_ids.shape[0]
    chosen = jnp.take(strain, case_ids, axis=0)
    rows = chosen.shape[2]

    packed = jnp.concatenate(
        [chosen.reshape(cases * 3, rows, col_local), stiffening, interface], axis=0
    )
    packed = with_halos(packed, "tile", 2, halo, halo)
    width = col_local + 2 * halo
    strain_e = packed[: cases * 3].reshape(cases, 3, rows, width)
    stiff_c = packed[cases * 3 : cases * 3 + ply_local]
    inter_c = packed[cases * 3 + ply_local :]
    angle_plane = jnp.zeros((1, rows, width), jnp.float32)
    below = passed_along(
        jnp.concatenate(
            [
                stiff_c[ply_local - halo :],
                inter_c[ply_local - halo - 1 :],
                angle_plane.at[0, 0, :halo].set(angle_ids[ply_local - halo :].astype(jnp.float32)),
            ],
            axis=0,
        ),
        "ply",
        1,
    )
    above = passed_along(
        jnp.concatenate(
            [
                stiff_c[:halo],
                inter_c[:halo],
                angle_plane.at[0, 0, :halo].set(angle_ids[:halo].astype(jnp.float32)),
            ],
            axis=0,
        ),
        "ply",
        -1,
    )
    angles = jnp.concatenate(
        [
            below[2 * halo + 1, 0, :halo].astype(jnp.int32),
            angle_ids,
            above[2 * halo, 0, :halo].astype(jnp.int32),
        ]
    )
    below = below[: 2 * halo + 1]
    above = above[: 2 * halo]
    stiff_e = jnp.concatenate([below[:halo], stiff_c, above[:halo]], axis=0)
    inter_all = jnp.concatenate([below[halo:], inter_c, above[halo:]], axis=0)
    up_e = inter_all[1:]
    down_e = inter_all[:-1]

    cond_rows, cond_cols, cond_cross, ply_cosine, ply_sine = ply_tables(angles)
    source_e = tsai_wu(
        strain_e[:, 0][:, None],
        strain_e[:, 1][:, None],
        strain_e[:, 2][:, None],
        ply_cosine,
        ply_sine,
    )
    ply_at = lax.axis_index("ply") * ply_local - halo + jnp.arange(ply_local + 2 * halo)
    col_at = lax.axis_index("tile") * col_local - halo + jnp.arange(width)
    inside = (
        ((ply_at >= 0) & (ply_at < ply_local * ply_count))[:, None, None]
        & ((col_at >= 0) & (col_at < col_local * tile_count))[None, None, :]
    ).astype(jnp.float32)

    diagonal_sum = 2.0 * cond_rows + 2.0 * cond_cols + up_e + down_e + stiff_e
    scale = relaxation / diagonal_sum
    forced = relaxation * source_e / diagonal_sum
    scale_up = scale * up_e
    scale_down = scale * down_e
    half_cross = 0.5 * cond_cross
    adjoint = forced * inside
    for iteration in range(1, ITERS):
        framed = jnp.pad(adjoint, ((0, 0), (1, 1), (1, 1), (1, 1)))
        centre = framed[:, 1:-1, 1:-1, 1:-1]
        along_rows = framed[:, 1:-1, 2:, 1:-1] + framed[:, 1:-1, :-2, 1:-1]
        along_cols = framed[:, 1:-1, 1:-1, 2:] + framed[:, 1:-1, 1:-1, :-2]
        diagonal_pairs = (
            framed[:, 1:-1, 2:, 2:]
            + framed[:, 1:-1, :-2, :-2]
            - framed[:, 1:-1, 2:, :-2]
            - framed[:, 1:-1, :-2, 2:]
        )
        overhead = framed[:, 2:, 1:-1, 1:-1]
        beneath = framed[:, :-2, 1:-1, 1:-1]
        in_plane = cond_rows * along_rows + cond_cols * along_cols + half_cross * diagonal_pairs
        adjoint = (
            (1.0 - relaxation) * centre
            + forced
            + scale * in_plane
            + scale_up * overhead
            + scale_down * beneath
        )
        if iteration < ITERS - 1:
            adjoint = adjoint * inside
    adjoint = trim(adjoint, halo, 1, 3)
    source = trim(source_e, halo, 1, 3)
    product = adjoint * source
    total = jnp.sum(product, axis=(0, 1))
    totals = lax.all_to_all(
        jnp.broadcast_to(total[None], (ply_count,) + total.shape), "ply", 0, 0, tiled=True
    )
    lower = (jnp.arange(ply_count) < lax.axis_index("ply")).astype(jnp.float32)
    prefix = jnp.sum(totals * lower[:, None, None], axis=0)
    running = jnp.cumsum(jnp.sum(product, axis=0), axis=0)
    through = (running + prefix[None]) / (ply_local * ply_count)
    return (adjoint, through)


def solution(mesh):
    return jax.shard_map(
        body,
        mesh=mesh,
        in_specs=(
            P(None, None, None, "tile"),
            P(),
            P("ply"),
            P("ply", None, "tile"),
            P("ply", None, "tile"),
        ),
        out_specs=(P(None, "ply", None, "tile"), P("ply", None, "tile")),
        check_vma=False,
    )
```

```python
import jax
import jax.numpy as jnp
from jax import lax
from jax.sharding import PartitionSpec as P
from jax.experimental import pallas as pl
from jax.experimental.pallas import tpu as pltpu

ITERS = 4


relaxation = 2.0 / 3.0
half_root = 0.7071067811865476
fibre_modulus = 1.0
trans_modulus = 0.5
shear_modulus = 0.3
linear_fibre = 0.3
linear_trans = 0.8
square_fibre = 0.5
square_trans = 1.0
square_shear = 0.8
cross_term = -0.35


def passed_along(array, axis, by):
    count = lax.axis_size(axis)
    pairs = [(i, i + by) for i in range(count) if 0 <= i + by < count]
    return lax.ppermute(array, axis, pairs)


def with_halos(block, axis, dim, below, above):
    size = block.shape[dim]
    low = passed_along(lax.slice_in_dim(block, size - below, size, axis=dim), axis, 1)
    high = passed_along(lax.slice_in_dim(block, 0, above, axis=dim), axis, -1)
    return jnp.concatenate([low, block, high], axis=dim)


def ply_tables(angles):
    one_hot = (angles[:, None] == jnp.arange(4, dtype=jnp.int32)[None, :]).astype(jnp.float32)
    ply_cosine = jnp.sum(
        one_hot * jnp.array([1.0, half_root, half_root, 0.0], jnp.float32)[None, :], axis=1
    )
    ply_sine = jnp.sum(
        one_hot * jnp.array([0.0, half_root, -half_root, 1.0], jnp.float32)[None, :], axis=1
    )
    ply_cosine = ply_cosine.reshape(-1, 1, 1)
    ply_sine = ply_sine.reshape(-1, 1, 1)
    cond_rows = 4.0 * ply_cosine * ply_cosine + ply_sine * ply_sine
    cond_cols = 4.0 * ply_sine * ply_sine + ply_cosine * ply_cosine
    cond_cross = 3.0 * ply_cosine * ply_sine
    return (cond_rows, cond_cols, cond_cross, ply_cosine, ply_sine)


def tsai_wu(strain_x, strain_y, strain_xy, ply_cosine, ply_sine):
    cos_sq = ply_cosine * ply_cosine
    sin_sq = ply_sine * ply_sine
    mixed = ply_cosine * ply_sine
    fibre_strain = cos_sq * strain_x + sin_sq * strain_y + mixed * strain_xy
    trans_strain = sin_sq * strain_x + cos_sq * strain_y - mixed * strain_xy
    shear_strain = 2.0 * mixed * (strain_y - strain_x) + (cos_sq - sin_sq) * strain_xy
    fibre_stress = fibre_modulus * fibre_strain
    trans_stress = trans_modulus * trans_strain
    shear_stress = shear_modulus * shear_strain
    first = linear_fibre + 2.0 * square_fibre * fibre_stress + 2.0 * cross_term * trans_stress
    second = linear_trans + 2.0 * square_trans * trans_stress + 2.0 * cross_term * fibre_stress
    return first + second + 2.0 * square_shear * shear_stress


def sweep(padded, source, stiffening, coupling_up, coupling_down, cond_rows, cond_cols, cond_cross):
    widths = [(0, 0)] * (padded.ndim - 2) + [(1, 1), (0, 0)]
    framed = jnp.pad(padded, widths)
    centre = framed[..., 1:-1, 1:-1, 1:-1]
    along_rows = framed[..., 1:-1, 2:, 1:-1] + framed[..., 1:-1, :-2, 1:-1]
    along_cols = framed[..., 1:-1, 1:-1, 2:] + framed[..., 1:-1, 1:-1, :-2]
    diagonal_pairs = (
        framed[..., 1:-1, 2:, 2:]
        + framed[..., 1:-1, :-2, :-2]
        - framed[..., 1:-1, 2:, :-2]
        - framed[..., 1:-1, :-2, 2:]
    )
    overhead = framed[..., 2:, 1:-1, 1:-1]
    beneath = framed[..., :-2, 1:-1, 1:-1]
    image = (
        cond_rows * (2.0 * centre - along_rows)
        + cond_cols * (2.0 * centre - along_cols)
        - 0.5 * cond_cross * diagonal_pairs
    )
    image = (
        image
        + coupling_up * (centre - overhead)
        + coupling_down * (centre - beneath)
        + stiffening * centre
    )
    diagonal_sum = 2.0 * cond_rows + 2.0 * cond_cols + coupling_up + coupling_down + stiffening
    return centre + relaxation * (source - image) / diagonal_sum


def sweeps_kernel(tab, ply_mask, strain_ref, stiff_ref, inter_ref, col_mask_ref, adj_ref, acc_ref, src_s, a_s, b_s):
    case = pl.program_id(0)
    planes, rows, lanes = stiff_ref.shape
    halo = ITERS - 1
    own_planes, own_cols = acc_ref.shape[0], acc_ref.shape[2]
    col_mask = col_mask_ref[...]
    row = lax.broadcasted_iota(jnp.int32, (rows, lanes), 0)
    keep_a = (jnp.abs(pltpu.roll(row, 1, 0) - row) == 1).astype(jnp.float32)
    keep_b = (jnp.abs(pltpu.roll(row, rows - 1, 0) - row) == 1).astype(jnp.float32)
    strain_x = strain_ref[0, 0]
    strain_y = strain_ref[0, 1]
    strain_xy = strain_ref[0, 2]

    def diagonal_at(p):
        cond_rows, cond_cols = tab[0, p], tab[1, p]
        return 2.0 * cond_rows + 2.0 * cond_cols + inter_ref[p + 1] + inter_ref[p] + stiff_ref[p]

    def first(p, carry):
        source = tsai_wu(strain_x, strain_y, strain_xy, tab[3, p], tab[4, p])
        src_s[p] = source
        a_s[p] = relaxation * source / diagonal_at(p) * (ply_mask[p] * col_mask)
        return carry

    lax.fori_loop(0, planes, first, 0)
    buffers = (a_s, b_s)
    for iteration in range(1, ITERS):
        previous, following = buffers[(iteration - 1) % 2], buffers[iteration % 2]
        masked = iteration < ITERS - 1

        def step(p, carry, previous=previous, following=following, masked=masked):
            centre = previous[p]
            row_a = pltpu.roll(centre, 1, 0) * keep_a
            row_b = pltpu.roll(centre, rows - 1, 0) * keep_b
            along_rows = row_a + row_b
            along_cols = pltpu.roll(centre, 1, 1) + pltpu.roll(centre, lanes - 1, 1)
            diagonal_pairs = (
                pltpu.roll(row_a, 1, 1)
                + pltpu.roll(row_b, lanes - 1, 1)
                - pltpu.roll(row_a, lanes - 1, 1)
                - pltpu.roll(row_b, 1, 1)
            )
            cond_rows, cond_cols, cond_cross = tab[0, p], tab[1, p], tab[2, p]
            coupling_up = inter_ref[p + 1]
            coupling_down = inter_ref[p]
            stiffening = stiff_ref[p]
            image = (
                cond_rows * (2.0 * centre - along_rows)
                + cond_cols * (2.0 * centre - along_cols)
                - 0.5 * cond_cross * diagonal_pairs
            )
            image = (
                image
                + coupling_up * (centre - previous[p + 1])
                + coupling_down * (centre - previous[p - 1])
                + stiffening * centre
            )
            diagonal_sum = 2.0 * cond_rows + 2.0 * cond_cols + coupling_up + coupling_down + stiffening
            value = centre + relaxation * (src_s[p] - image) / diagonal_sum
            if masked:
                value = value * (ply_mask[p] * col_mask)
            following[p] = value
            return carry

        lax.fori_loop(iteration, planes - iteration, step, 0)
    final = buffers[(ITERS - 1) % 2]

    @pl.when(case == 0)
    def _():
        acc_ref[...] = jnp.zeros(acc_ref.shape, jnp.float32)

    def store(p, carry):
        value = final[p + halo][:, :own_cols]
        adj_ref[0, p] = value
        acc_ref[p] = acc_ref[p] + value * src_s[p + halo][:, :own_cols]
        return carry

    lax.fori_loop(0, own_planes, store, 0)


def trim(array, by, ply_dim, col_dim):
    if by == 0:
        return array
    array = lax.slice_in_dim(array, by, array.shape[ply_dim] - by, axis=ply_dim)
    return lax.slice_in_dim(array, by, array.shape[col_dim] - by, axis=col_dim)


def body(strain, case_ids, angle_ids, stiffening, interface):
    halo = ITERS - 1
    ply_local = angle_ids.shape[0]
    col_local = stiffening.shape[2]
    ply_count = lax.axis_size("ply")
    tile_count = lax.axis_size("tile")
    cases = case_ids.shape[0]
    chosen = jnp.take(strain, case_ids, axis=0)
    rows = chosen.shape[2]

    lanes = -(-(col_local + 2 * halo) // 128) * 128
    flat = jnp.concatenate(
        [chosen.reshape(cases * 3, rows, col_local), stiffening, interface], axis=0
    )
    left = passed_along(flat[..., col_local - halo :], "tile", 1)
    right = passed_along(flat[..., :halo], "tile", -1)
    gap = jnp.zeros(flat.shape[:2] + (lanes - col_local - 2 * halo,), jnp.float32)
    packed = jnp.concatenate([flat, right, gap, left], axis=2)
    strain_e = packed[: cases * 3].reshape(cases, 3, rows, lanes)
    stiff_c = packed[cases * 3 : cases * 3 + ply_local]
    inter_c = packed[cases * 3 + ply_local :]
    angle_plane = jnp.zeros((1, rows, lanes), jnp.float32)
    below = passed_along(
        jnp.concatenate(
            [
                stiff_c[ply_local - halo :],
                inter_c[ply_local - halo - 1 :],
                angle_plane.at[0, 0, :halo].set(angle_ids[ply_local - halo :].astype(jnp.float32)),
            ],
            axis=0,
        ),
        "ply",
        1,
    )
    above = passed_along(
        jnp.concatenate(
            [
                stiff_c[:halo],
                inter_c[:halo],
                angle_plane.at[0, 0, :halo].set(angle_ids[:halo].astype(jnp.float32)),
            ],
            axis=0,
        ),
        "ply",
        -1,
    )
    angles = jnp.concatenate(
        [
            below[2 * halo + 1, 0, :halo].astype(jnp.int32),
            angle_ids,
            above[2 * halo, 0, :halo].astype(jnp.int32),
        ]
    )
    stiff_e = jnp.concatenate([below[:halo], stiff_c, above[:halo]], axis=0)
    inter_all = jnp.concatenate([below[halo : 2 * halo + 1], inter_c, above[halo : 2 * halo]], axis=0)

    cond_rows, cond_cols, cond_cross, ply_cosine, ply_sine = ply_tables(angles)
    tab = jnp.stack(
        [t.reshape(-1) for t in (cond_rows, cond_cols, cond_cross, ply_cosine, ply_sine)]
    )
    planes = ply_local + 2 * halo
    ply_at = lax.axis_index("ply") * ply_local - halo + jnp.arange(planes)
    ply_mask = ((ply_at >= 0) & (ply_at < ply_local * ply_count)).astype(jnp.float32)
    lane = jnp.arange(lanes)
    col_at = lax.axis_index("tile") * col_local + jnp.where(lane >= lanes - halo, lane - lanes, lane)
    col_ok = (lane < col_local + halo) | (lane >= lanes - halo)
    col_ok = col_ok & (col_at >= 0) & (col_at < col_local * tile_count)
    col_mask = jnp.broadcast_to(col_ok.astype(jnp.float32)[None, :], (rows, lanes))

    adjoint, summed = pl.pallas_call(
        sweeps_kernel,
        grid=(cases,),
        in_specs=[
            pl.BlockSpec(memory_space=pltpu.SMEM),
            pl.BlockSpec(memory_space=pltpu.SMEM),
            pl.BlockSpec((1, 3, rows, lanes), lambda c: (c, 0, 0, 0)),
            pl.BlockSpec((planes, rows, lanes), lambda c: (0, 0, 0)),
            pl.BlockSpec((planes + 1, rows, lanes), lambda c: (0, 0, 0)),
            pl.BlockSpec((rows, lanes), lambda c: (0, 0)),
        ],
        out_specs=[
            pl.BlockSpec((1, ply_local, rows, col_local), lambda c: (c, 0, 0, 0)),
            pl.BlockSpec((ply_local, rows, col_local), lambda c: (0, 0, 0)),
        ],
        out_shape=[
            jax.ShapeDtypeStruct((cases, ply_local, rows, col_local), jnp.float32),
            jax.ShapeDtypeStruct((ply_local, rows, col_local), jnp.float32),
        ],
        scratch_shapes=[pltpu.VMEM((planes, rows, lanes), jnp.float32)] * 3,
        compiler_params=pltpu.CompilerParams(dimension_semantics=("arbitrary",)),
    )(tab, ply_mask, strain_e, stiff_e, inter_all, col_mask)
    total = jnp.sum(summed, axis=0)
    totals = lax.all_to_all(
        jnp.broadcast_to(total[None], (ply_count,) + total.shape), "ply", 0, 0, tiled=True
    )
    lower = (jnp.arange(ply_count) < lax.axis_index("ply")).astype(jnp.float32)
    prefix = jnp.sum(totals * lower[:, None, None], axis=0)
    running = jnp.cumsum(summed, axis=0)
    through = (running + prefix[None]) / (ply_local * ply_count)
    return (adjoint, through)


def solution(mesh):
    return jax.shard_map(
        body,
        mesh=mesh,
        in_specs=(
            P(None, None, None, "tile"),
            P(),
            P("ply"),
            P("ply", None, "tile"),
            P("ply", None, "tile"),
        ),
        out_specs=(P(None, "ply", None, "tile"), P("ply", None, "tile")),
        check_vma=False,
    )
```

```python
import jax
import jax.numpy as jnp
from jax import lax
from jax.sharding import PartitionSpec as P
from jax.experimental import pallas as pl
from jax.experimental.pallas import tpu as pltpu

ITERS = 4


relaxation = 2.0 / 3.0
half_root = 0.7071067811865476
fibre_modulus = 1.0
trans_modulus = 0.5
shear_modulus = 0.3
linear_fibre = 0.3
linear_trans = 0.8
square_fibre = 0.5
square_trans = 1.0
square_shear = 0.8
cross_term = -0.35


def passed_along(array, axis, by):
    count = lax.axis_size(axis)
    pairs = [(i, i + by) for i in range(count) if 0 <= i + by < count]
    return lax.ppermute(array, axis, pairs)


def with_halos(block, axis, dim, below, above):
    size = block.shape[dim]
    low = passed_along(lax.slice_in_dim(block, size - below, size, axis=dim), axis, 1)
    high = passed_along(lax.slice_in_dim(block, 0, above, axis=dim), axis, -1)
    return jnp.concatenate([low, block, high], axis=dim)


def ply_tables(angles):
    one_hot = (angles[:, None] == jnp.arange(4, dtype=jnp.int32)[None, :]).astype(jnp.float32)
    ply_cosine = jnp.sum(
        one_hot * jnp.array([1.0, half_root, half_root, 0.0], jnp.float32)[None, :], axis=1
    )
    ply_sine = jnp.sum(
        one_hot * jnp.array([0.0, half_root, -half_root, 1.0], jnp.float32)[None, :], axis=1
    )
    ply_cosine = ply_cosine.reshape(-1, 1, 1)
    ply_sine = ply_sine.reshape(-1, 1, 1)
    cond_rows = 4.0 * ply_cosine * ply_cosine + ply_sine * ply_sine
    cond_cols = 4.0 * ply_sine * ply_sine + ply_cosine * ply_cosine
    cond_cross = 3.0 * ply_cosine * ply_sine
    return (cond_rows, cond_cols, cond_cross, ply_cosine, ply_sine)


def tsai_wu(strain_x, strain_y, strain_xy, ply_cosine, ply_sine):
    cos_sq = ply_cosine * ply_cosine
    sin_sq = ply_sine * ply_sine
    mixed = ply_cosine * ply_sine
    fibre_strain = cos_sq * strain_x + sin_sq * strain_y + mixed * strain_xy
    trans_strain = sin_sq * strain_x + cos_sq * strain_y - mixed * strain_xy
    shear_strain = 2.0 * mixed * (strain_y - strain_x) + (cos_sq - sin_sq) * strain_xy
    fibre_stress = fibre_modulus * fibre_strain
    trans_stress = trans_modulus * trans_strain
    shear_stress = shear_modulus * shear_strain
    first = linear_fibre + 2.0 * square_fibre * fibre_stress + 2.0 * cross_term * trans_stress
    second = linear_trans + 2.0 * square_trans * trans_stress + 2.0 * cross_term * fibre_stress
    return first + second + 2.0 * square_shear * shear_stress


def sweep(padded, source, stiffening, coupling_up, coupling_down, cond_rows, cond_cols, cond_cross):
    widths = [(0, 0)] * (padded.ndim - 2) + [(1, 1), (0, 0)]
    framed = jnp.pad(padded, widths)
    centre = framed[..., 1:-1, 1:-1, 1:-1]
    along_rows = framed[..., 1:-1, 2:, 1:-1] + framed[..., 1:-1, :-2, 1:-1]
    along_cols = framed[..., 1:-1, 1:-1, 2:] + framed[..., 1:-1, 1:-1, :-2]
    diagonal_pairs = (
        framed[..., 1:-1, 2:, 2:]
        + framed[..., 1:-1, :-2, :-2]
        - framed[..., 1:-1, 2:, :-2]
        - framed[..., 1:-1, :-2, 2:]
    )
    overhead = framed[..., 2:, 1:-1, 1:-1]
    beneath = framed[..., :-2, 1:-1, 1:-1]
    image = (
        cond_rows * (2.0 * centre - along_rows)
        + cond_cols * (2.0 * centre - along_cols)
        - 0.5 * cond_cross * diagonal_pairs
    )
    image = (
        image
        + coupling_up * (centre - overhead)
        + coupling_down * (centre - beneath)
        + stiffening * centre
    )
    diagonal_sum = 2.0 * cond_rows + 2.0 * cond_cols + coupling_up + coupling_down + stiffening
    return centre + relaxation * (source - image) / diagonal_sum


def sweeps_kernel(
    tab, ply_mask, strain_ref, stiff_ref, inter_ref, col_mask_ref, adj_ref, acc_ref,
    src_s, forced_s, scale_s, up_s, down_s, a_s, b_s,
):
    case = pl.program_id(0)
    planes, rows, lanes = stiff_ref.shape
    halo = ITERS - 1
    own_planes, own_cols = acc_ref.shape[0], acc_ref.shape[2]
    col_mask = col_mask_ref[...]
    row = lax.broadcasted_iota(jnp.int32, (rows, lanes), 0)
    keep_a = (jnp.abs(pltpu.roll(row, 1, 0) - row) == 1).astype(jnp.float32)
    keep_b = (jnp.abs(pltpu.roll(row, rows - 1, 0) - row) == 1).astype(jnp.float32)
    strain_x = strain_ref[0, 0]
    strain_y = strain_ref[0, 1]
    strain_xy = strain_ref[0, 2]

    def diagonal_at(p):
        cond_rows, cond_cols = tab[0, p], tab[1, p]
        return 2.0 * cond_rows + 2.0 * cond_cols + inter_ref[p + 1] + inter_ref[p] + stiff_ref[p]

    @pl.when(case == 0)
    def _():
        def scales(p, carry):
            scale = relaxation / diagonal_at(p)
            scale_s[p] = scale
            up_s[p] = scale * inter_ref[p + 1]
            down_s[p] = scale * inter_ref[p]
            return carry

        lax.fori_loop(0, planes, scales, 0)
        acc_ref[...] = jnp.zeros(acc_ref.shape, jnp.float32)

    def first(p, carry):
        source = tsai_wu(strain_x, strain_y, strain_xy, tab[3, p], tab[4, p])
        forced = relaxation * source / diagonal_at(p)
        src_s[p] = source
        forced_s[p] = forced
        a_s[p] = forced * (ply_mask[p] * col_mask)
        return carry

    lax.fori_loop(0, planes, first, 0)
    buffers = (a_s, b_s)
    for iteration in range(1, ITERS):
        previous, following = buffers[(iteration - 1) % 2], buffers[iteration % 2]
        masked = iteration < ITERS - 1

        def step(p, carry, previous=previous, following=following, masked=masked):
            centre = previous[p]
            row_a = pltpu.roll(centre, 1, 0) * keep_a
            row_b = pltpu.roll(centre, rows - 1, 0) * keep_b
            along_rows = row_a + row_b
            along_cols = pltpu.roll(centre, 1, 1) + pltpu.roll(centre, lanes - 1, 1)
            diagonal_pairs = (
                pltpu.roll(row_a, 1, 1)
                + pltpu.roll(row_b, lanes - 1, 1)
                - pltpu.roll(row_a, lanes - 1, 1)
                - pltpu.roll(row_b, 1, 1)
            )
            in_plane = (
                tab[0, p] * along_rows + tab[1, p] * along_cols + (0.5 * tab[2, p]) * diagonal_pairs
            )
            value = (
                (1.0 - relaxation) * centre
                + forced_s[p]
                + scale_s[p] * in_plane
                + up_s[p] * previous[p + 1]
                + down_s[p] * previous[p - 1]
            )
            if masked:
                value = value * (ply_mask[p] * col_mask)
            following[p] = value
            return carry

        lax.fori_loop(iteration, planes - iteration, step, 0, unroll=2)
    final = buffers[(ITERS - 1) % 2]

    def store(p, carry):
        value = final[p + halo][:, :own_cols]
        adj_ref[0, p] = value
        acc_ref[p] = acc_ref[p] + value * src_s[p + halo][:, :own_cols]
        return carry

    lax.fori_loop(0, own_planes, store, 0)


def trim(array, by, ply_dim, col_dim):
    if by == 0:
        return array
    array = lax.slice_in_dim(array, by, array.shape[ply_dim] - by, axis=ply_dim)
    return lax.slice_in_dim(array, by, array.shape[col_dim] - by, axis=col_dim)


def body(strain, case_ids, angle_ids, stiffening, interface):
    halo = ITERS - 1
    ply_local = angle_ids.shape[0]
    col_local = stiffening.shape[2]
    ply_count = lax.axis_size("ply")
    tile_count = lax.axis_size("tile")
    cases = case_ids.shape[0]
    chosen = jnp.take(strain, case_ids, axis=0)
    rows = chosen.shape[2]

    lanes = -(-(col_local + 2 * halo) // 128) * 128
    flat = jnp.concatenate(
        [chosen.reshape(cases * 3, rows, col_local), stiffening, interface], axis=0
    )
    left = passed_along(flat[..., col_local - halo :], "tile", 1)
    right = passed_along(flat[..., :halo], "tile", -1)
    gap = jnp.zeros(flat.shape[:2] + (lanes - col_local - 2 * halo,), jnp.float32)
    packed = jnp.concatenate([flat, right, gap, left], axis=2)
    strain_e = packed[: cases * 3].reshape(cases, 3, rows, lanes)
    stiff_c = packed[cases * 3 : cases * 3 + ply_local]
    inter_c = packed[cases * 3 + ply_local :]
    angle_plane = jnp.zeros((1, rows, lanes), jnp.float32)
    below = passed_along(
        jnp.concatenate(
            [
                stiff_c[ply_local - halo :],
                inter_c[ply_local - halo - 1 :],
                angle_plane.at[0, 0, :halo].set(angle_ids[ply_local - halo :].astype(jnp.float32)),
            ],
            axis=0,
        ),
        "ply",
        1,
    )
    above = passed_along(
        jnp.concatenate(
            [
                stiff_c[:halo],
                inter_c[:halo],
                angle_plane.at[0, 0, :halo].set(angle_ids[:halo].astype(jnp.float32)),
            ],
            axis=0,
        ),
        "ply",
        -1,
    )
    angles = jnp.concatenate(
        [
            below[2 * halo + 1, 0, :halo].astype(jnp.int32),
            angle_ids,
            above[2 * halo, 0, :halo].astype(jnp.int32),
        ]
    )
    stiff_e = jnp.concatenate([below[:halo], stiff_c, above[:halo]], axis=0)
    inter_all = jnp.concatenate([below[halo : 2 * halo + 1], inter_c, above[halo : 2 * halo]], axis=0)

    cond_rows, cond_cols, cond_cross, ply_cosine, ply_sine = ply_tables(angles)
    tab = jnp.stack(
        [t.reshape(-1) for t in (cond_rows, cond_cols, cond_cross, ply_cosine, ply_sine)]
    )
    planes = ply_local + 2 * halo
    ply_at = lax.axis_index("ply") * ply_local - halo + jnp.arange(planes)
    ply_mask = ((ply_at >= 0) & (ply_at < ply_local * ply_count)).astype(jnp.float32)
    lane = jnp.arange(lanes)
    col_at = lax.axis_index("tile") * col_local + jnp.where(lane >= lanes - halo, lane - lanes, lane)
    col_ok = (lane < col_local + halo) | (lane >= lanes - halo)
    col_ok = col_ok & (col_at >= 0) & (col_at < col_local * tile_count)
    col_mask = jnp.broadcast_to(col_ok.astype(jnp.float32)[None, :], (rows, lanes))

    adjoint, summed = pl.pallas_call(
        sweeps_kernel,
        grid=(cases,),
        in_specs=[
            pl.BlockSpec(memory_space=pltpu.SMEM),
            pl.BlockSpec(memory_space=pltpu.SMEM),
            pl.BlockSpec((1, 3, rows, lanes), lambda c: (c, 0, 0, 0)),
            pl.BlockSpec((planes, rows, lanes), lambda c: (0, 0, 0)),
            pl.BlockSpec((planes + 1, rows, lanes), lambda c: (0, 0, 0)),
            pl.BlockSpec((rows, lanes), lambda c: (0, 0)),
        ],
        out_specs=[
            pl.BlockSpec((1, ply_local, rows, col_local), lambda c: (c, 0, 0, 0)),
            pl.BlockSpec((ply_local, rows, col_local), lambda c: (0, 0, 0)),
        ],
        out_shape=[
            jax.ShapeDtypeStruct((cases, ply_local, rows, col_local), jnp.float32),
            jax.ShapeDtypeStruct((ply_local, rows, col_local), jnp.float32),
        ],
        scratch_shapes=[pltpu.VMEM((planes, rows, lanes), jnp.float32)] * 7,
        compiler_params=pltpu.CompilerParams(dimension_semantics=("arbitrary",)),
    )(tab, ply_mask, strain_e, stiff_e, inter_all, col_mask)
    total = jnp.sum(summed, axis=0)
    totals = lax.all_to_all(
        jnp.broadcast_to(total[None], (ply_count,) + total.shape), "ply", 0, 0, tiled=True
    )
    lower = (jnp.arange(ply_count) < lax.axis_index("ply")).astype(jnp.float32)
    prefix = jnp.sum(totals * lower[:, None, None], axis=0)
    running = jnp.cumsum(summed, axis=0)
    through = (running + prefix[None]) / (ply_local * ply_count)
    return (adjoint, through)


def solution(mesh):
    return jax.shard_map(
        body,
        mesh=mesh,
        in_specs=(
            P(None, None, None, "tile"),
            P(),
            P("ply"),
            P("ply", None, "tile"),
            P("ply", None, "tile"),
        ),
        out_specs=(P(None, "ply", None, "tile"), P("ply", None, "tile")),
        check_vma=False,
    )
```

```python
import jax
import jax.numpy as jnp
from jax import lax
from jax.sharding import PartitionSpec as P

ITERS = 4


relaxation = 2.0 / 3.0
half_root = 0.7071067811865476
fibre_modulus = 1.0
trans_modulus = 0.5
shear_modulus = 0.3
linear_fibre = 0.3
linear_trans = 0.8
square_fibre = 0.5
square_trans = 1.0
square_shear = 0.8
cross_term = -0.35


def passed_along(array, axis, by):
    count = lax.axis_size(axis)
    pairs = [(i, i + by) for i in range(count) if 0 <= i + by < count]
    return lax.ppermute(array, axis, pairs)


def with_halos(block, axis, dim, below, above):
    size = block.shape[dim]
    low = passed_along(lax.slice_in_dim(block, size - below, size, axis=dim), axis, 1)
    high = passed_along(lax.slice_in_dim(block, 0, above, axis=dim), axis, -1)
    return jnp.concatenate([low, block, high], axis=dim)


def ply_tables(angles):
    one_hot = (angles[:, None] == jnp.arange(4, dtype=jnp.int32)[None, :]).astype(jnp.float32)
    ply_cosine = jnp.sum(
        one_hot * jnp.array([1.0, half_root, half_root, 0.0], jnp.float32)[None, :], axis=1
    )
    ply_sine = jnp.sum(
        one_hot * jnp.array([0.0, half_root, -half_root, 1.0], jnp.float32)[None, :], axis=1
    )
    ply_cosine = ply_cosine.reshape(-1, 1, 1)
    ply_sine = ply_sine.reshape(-1, 1, 1)
    cond_rows = 4.0 * ply_cosine * ply_cosine + ply_sine * ply_sine
    cond_cols = 4.0 * ply_sine * ply_sine + ply_cosine * ply_cosine
    cond_cross = 3.0 * ply_cosine * ply_sine
    return (cond_rows, cond_cols, cond_cross, ply_cosine, ply_sine)


def tsai_wu(strain_x, strain_y, strain_xy, ply_cosine, ply_sine):
    cos_sq = ply_cosine * ply_cosine
    sin_sq = ply_sine * ply_sine
    mixed = ply_cosine * ply_sine
    fibre_strain = cos_sq * strain_x + sin_sq * strain_y + mixed * strain_xy
    trans_strain = sin_sq * strain_x + cos_sq * strain_y - mixed * strain_xy
    shear_strain = 2.0 * mixed * (strain_y - strain_x) + (cos_sq - sin_sq) * strain_xy
    fibre_stress = fibre_modulus * fibre_strain
    trans_stress = trans_modulus * trans_strain
    shear_stress = shear_modulus * shear_strain
    first = linear_fibre + 2.0 * square_fibre * fibre_stress + 2.0 * cross_term * trans_stress
    second = linear_trans + 2.0 * square_trans * trans_stress + 2.0 * cross_term * fibre_stress
    return first + second + 2.0 * square_shear * shear_stress


def sweep(padded, source, stiffening, coupling_up, coupling_down, cond_rows, cond_cols, cond_cross):
    widths = [(0, 0)] * (padded.ndim - 2) + [(1, 1), (0, 0)]
    framed = jnp.pad(padded, widths)
    centre = framed[..., 1:-1, 1:-1, 1:-1]
    along_rows = framed[..., 1:-1, 2:, 1:-1] + framed[..., 1:-1, :-2, 1:-1]
    along_cols = framed[..., 1:-1, 1:-1, 2:] + framed[..., 1:-1, 1:-1, :-2]
    diagonal_pairs = (
        framed[..., 1:-1, 2:, 2:]
        + framed[..., 1:-1, :-2, :-2]
        - framed[..., 1:-1, 2:, :-2]
        - framed[..., 1:-1, :-2, 2:]
    )
    overhead = framed[..., 2:, 1:-1, 1:-1]
    beneath = framed[..., :-2, 1:-1, 1:-1]
    image = (
        cond_rows * (2.0 * centre - along_rows)
        + cond_cols * (2.0 * centre - along_cols)
        - 0.5 * cond_cross * diagonal_pairs
    )
    image = (
        image
        + coupling_up * (centre - overhead)
        + coupling_down * (centre - beneath)
        + stiffening * centre
    )
    diagonal_sum = 2.0 * cond_rows + 2.0 * cond_cols + coupling_up + coupling_down + stiffening
    return centre + relaxation * (source - image) / diagonal_sum


def trim(array, by, ply_dim, col_dim):
    if by == 0:
        return array
    array = lax.slice_in_dim(array, by, array.shape[ply_dim] - by, axis=ply_dim)
    return lax.slice_in_dim(array, by, array.shape[col_dim] - by, axis=col_dim)


def body(strain, case_ids, angle_ids, stiffening, interface):
    halo = ITERS - 1
    ply_local = angle_ids.shape[0]
    col_local = stiffening.shape[2]
    ply_count = lax.axis_size("ply")
    tile_count = lax.axis_size("tile")
    cases = case_ids.shape[0]
    rows = strain.shape[2]
    width = col_local + 2 * halo

    def edge(start):
        return jnp.concatenate(
            [
                lax.slice_in_dim(strain, start, start + halo, axis=3).reshape(-1, rows, halo),
                lax.slice_in_dim(stiffening, start, start + halo, axis=2),
                lax.slice_in_dim(interface, start, start + halo, axis=2),
            ],
            axis=0,
        )

    left = passed_along(edge(col_local - halo), "tile", 1)
    right = passed_along(edge(0), "tile", -1)
    states = strain.shape[0] * 3
    strain_all = jnp.concatenate(
        [
            left[:states].reshape(strain.shape[:3] + (halo,)),
            strain,
            right[:states].reshape(strain.shape[:3] + (halo,)),
        ],
        axis=3,
    )
    strain_e = jnp.take(strain_all, case_ids, axis=0)
    stiff_c = jnp.concatenate(
        [left[states : states + ply_local], stiffening, right[states : states + ply_local]], axis=2
    )
    inter_c = jnp.concatenate(
        [left[states + ply_local :], interface, right[states + ply_local :]], axis=2
    )
    angle_plane = jnp.zeros((1, rows, width), jnp.float32)
    below = passed_along(
        jnp.concatenate(
            [
                stiff_c[ply_local - halo :],
                inter_c[ply_local - halo - 1 :],
                angle_plane.at[0, 0, :halo].set(angle_ids[ply_local - halo :].astype(jnp.float32)),
            ],
            axis=0,
        ),
        "ply",
        1,
    )
    above = passed_along(
        jnp.concatenate(
            [
                stiff_c[:halo],
                inter_c[:halo],
                angle_plane.at[0, 0, :halo].set(angle_ids[:halo].astype(jnp.float32)),
            ],
            axis=0,
        ),
        "ply",
        -1,
    )
    angles = jnp.concatenate(
        [
            below[2 * halo + 1, 0, :halo].astype(jnp.int32),
            angle_ids,
            above[2 * halo, 0, :halo].astype(jnp.int32),
        ]
    )
    below = below[: 2 * halo + 1]
    above = above[: 2 * halo]
    stiff_e = jnp.concatenate([below[:halo], stiff_c, above[:halo]], axis=0)
    inter_all = jnp.concatenate([below[halo:], inter_c, above[halo:]], axis=0)
    up_e = inter_all[1:]
    down_e = inter_all[:-1]

    cond_rows, cond_cols, cond_cross, ply_cosine, ply_sine = ply_tables(angles)
    source_e = tsai_wu(
        strain_e[:, 0][:, None],
        strain_e[:, 1][:, None],
        strain_e[:, 2][:, None],
        ply_cosine,
        ply_sine,
    )
    ply_at = lax.axis_index("ply") * ply_local - halo + jnp.arange(ply_local + 2 * halo)
    col_at = lax.axis_index("tile") * col_local - halo + jnp.arange(width)
    inside = (
        ((ply_at >= 0) & (ply_at < ply_local * ply_count))[:, None, None]
        & ((col_at >= 0) & (col_at < col_local * tile_count))[None, None, :]
    ).astype(jnp.float32)

    diagonal_sum = 2.0 * cond_rows + 2.0 * cond_cols + up_e + down_e + stiff_e
    adjoint = relaxation * source_e / diagonal_sum * inside
    for iteration in range(1, ITERS):
        by = iteration
        adjoint = sweep(
            adjoint,
            trim(source_e, by, 1, 3),
            trim(stiff_e, by, 0, 2),
            trim(up_e, by, 0, 2),
            trim(down_e, by, 0, 2),
            cond_rows[by : cond_rows.shape[0] - by],
            cond_cols[by : cond_cols.shape[0] - by],
            cond_cross[by : cond_cross.shape[0] - by],
        )
        if iteration < ITERS - 1:
            adjoint = adjoint * trim(inside, by, 0, 2)
    source = trim(source_e, halo, 1, 3)
    product = adjoint * source
    total = jnp.sum(product, axis=(0, 1))
    totals = lax.all_to_all(
        jnp.broadcast_to(total[None], (ply_count,) + total.shape), "ply", 0, 0, tiled=True
    )
    lower = (jnp.arange(ply_count) < lax.axis_index("ply")).astype(jnp.float32)
    prefix = jnp.sum(totals * lower[:, None, None], axis=0)
    running = jnp.cumsum(jnp.sum(product, axis=0), axis=0)
    through = (running + prefix[None]) / (ply_local * ply_count)
    return (adjoint, through)


def solution(mesh):
    return jax.shard_map(
        body,
        mesh=mesh,
        in_specs=(
            P(None, None, None, "tile"),
            P(),
            P("ply"),
            P("ply", None, "tile"),
            P("ply", None, "tile"),
        ),
        out_specs=(P(None, "ply", None, "tile"), P("ply", None, "tile")),
        check_vma=False,
    )
```

```python
import jax
import jax.numpy as jnp
from jax import lax
from jax.sharding import PartitionSpec as P

ITERS = 4


relaxation = 2.0 / 3.0
half_root = 0.7071067811865476
fibre_modulus = 1.0
trans_modulus = 0.5
shear_modulus = 0.3
linear_fibre = 0.3
linear_trans = 0.8
square_fibre = 0.5
square_trans = 1.0
square_shear = 0.8
cross_term = -0.35


def passed_along(array, axis, by):
    count = lax.axis_size(axis)
    pairs = [(i, i + by) for i in range(count) if 0 <= i + by < count]
    return lax.ppermute(array, axis, pairs)


def with_halos(block, axis, dim, below, above):
    size = block.shape[dim]
    low = passed_along(lax.slice_in_dim(block, size - below, size, axis=dim), axis, 1)
    high = passed_along(lax.slice_in_dim(block, 0, above, axis=dim), axis, -1)
    return jnp.concatenate([low, block, high], axis=dim)


def ply_tables(angles):
    one_hot = (angles[:, None] == jnp.arange(4, dtype=jnp.int32)[None, :]).astype(jnp.float32)
    ply_cosine = jnp.sum(
        one_hot * jnp.array([1.0, half_root, half_root, 0.0], jnp.float32)[None, :], axis=1
    )
    ply_sine = jnp.sum(
        one_hot * jnp.array([0.0, half_root, -half_root, 1.0], jnp.float32)[None, :], axis=1
    )
    ply_cosine = ply_cosine.reshape(-1, 1, 1)
    ply_sine = ply_sine.reshape(-1, 1, 1)
    cond_rows = 4.0 * ply_cosine * ply_cosine + ply_sine * ply_sine
    cond_cols = 4.0 * ply_sine * ply_sine + ply_cosine * ply_cosine
    cond_cross = 3.0 * ply_cosine * ply_sine
    return (cond_rows, cond_cols, cond_cross, ply_cosine, ply_sine)


def tsai_wu(strain_x, strain_y, strain_xy, ply_cosine, ply_sine):
    cos_sq = ply_cosine * ply_cosine
    sin_sq = ply_sine * ply_sine
    mixed = ply_cosine * ply_sine
    fibre_strain = cos_sq * strain_x + sin_sq * strain_y + mixed * strain_xy
    trans_strain = sin_sq * strain_x + cos_sq * strain_y - mixed * strain_xy
    shear_strain = 2.0 * mixed * (strain_y - strain_x) + (cos_sq - sin_sq) * strain_xy
    fibre_stress = fibre_modulus * fibre_strain
    trans_stress = trans_modulus * trans_strain
    shear_stress = shear_modulus * shear_strain
    first = linear_fibre + 2.0 * square_fibre * fibre_stress + 2.0 * cross_term * trans_stress
    second = linear_trans + 2.0 * square_trans * trans_stress + 2.0 * cross_term * fibre_stress
    return first + second + 2.0 * square_shear * shear_stress


def sweep(padded, source, stiffening, coupling_up, coupling_down, cond_rows, cond_cols, cond_cross):
    widths = [(0, 0)] * (padded.ndim - 2) + [(1, 1), (0, 0)]
    framed = jnp.pad(padded, widths)
    centre = framed[..., 1:-1, 1:-1, 1:-1]
    along_rows = framed[..., 1:-1, 2:, 1:-1] + framed[..., 1:-1, :-2, 1:-1]
    along_cols = framed[..., 1:-1, 1:-1, 2:] + framed[..., 1:-1, 1:-1, :-2]
    diagonal_pairs = (
        framed[..., 1:-1, 2:, 2:]
        + framed[..., 1:-1, :-2, :-2]
        - framed[..., 1:-1, 2:, :-2]
        - framed[..., 1:-1, :-2, 2:]
    )
    overhead = framed[..., 2:, 1:-1, 1:-1]
    beneath = framed[..., :-2, 1:-1, 1:-1]
    image = (
        cond_rows * (2.0 * centre - along_rows)
        + cond_cols * (2.0 * centre - along_cols)
        - 0.5 * cond_cross * diagonal_pairs
    )
    image = (
        image
        + coupling_up * (centre - overhead)
        + coupling_down * (centre - beneath)
        + stiffening * centre
    )
    diagonal_sum = 2.0 * cond_rows + 2.0 * cond_cols + coupling_up + coupling_down + stiffening
    return centre + relaxation * (source - image) / diagonal_sum


def trim(array, by, ply_dim, col_dim):
    if by == 0:
        return array
    array = lax.slice_in_dim(array, by, array.shape[ply_dim] - by, axis=ply_dim)
    return lax.slice_in_dim(array, by, array.shape[col_dim] - by, axis=col_dim)


def body(strain, case_ids, angle_ids, stiffening, interface):
    halo = ITERS - 1
    ply_local = angle_ids.shape[0]
    col_local = stiffening.shape[2]
    ply_count = lax.axis_size("ply")
    tile_count = lax.axis_size("tile")
    cases = case_ids.shape[0]
    rows = strain.shape[2]
    width = col_local + 2 * halo

    def edge(start):
        return jnp.concatenate(
            [
                lax.slice_in_dim(strain, start, start + halo, axis=3).reshape(-1, rows, halo),
                lax.slice_in_dim(stiffening, start, start + halo, axis=2),
                lax.slice_in_dim(interface, start, start + halo, axis=2),
            ],
            axis=0,
        )

    left = passed_along(edge(col_local - halo), "tile", 1)
    right = passed_along(edge(0), "tile", -1)
    states = strain.shape[0] * 3
    strain_all = jnp.concatenate(
        [
            left[:states].reshape(strain.shape[:3] + (halo,)),
            strain,
            right[:states].reshape(strain.shape[:3] + (halo,)),
        ],
        axis=3,
    )
    strain_e = jnp.take(strain_all, case_ids, axis=0)
    stiff_c = jnp.concatenate(
        [left[states : states + ply_local], stiffening, right[states : states + ply_local]], axis=2
    )
    inter_c = jnp.concatenate(
        [left[states + ply_local :], interface, right[states + ply_local :]], axis=2
    )
    angle_plane = jnp.zeros((1, rows, width), jnp.float32)
    below = passed_along(
        jnp.concatenate(
            [
                stiff_c[ply_local - halo :],
                inter_c[ply_local - halo - 1 :],
                angle_plane.at[0, 0, :halo].set(angle_ids[ply_local - halo :].astype(jnp.float32)),
            ],
            axis=0,
        ),
        "ply",
        1,
    )
    above = passed_along(
        jnp.concatenate(
            [
                stiff_c[:halo],
                inter_c[:halo],
                angle_plane.at[0, 0, :halo].set(angle_ids[:halo].astype(jnp.float32)),
            ],
            axis=0,
        ),
        "ply",
        -1,
    )
    angles = jnp.concatenate(
        [
            below[2 * halo + 1, 0, :halo].astype(jnp.int32),
            angle_ids,
            above[2 * halo, 0, :halo].astype(jnp.int32),
        ]
    )
    below = below[: 2 * halo + 1]
    above = above[: 2 * halo]
    stiff_e = jnp.concatenate([below[:halo], stiff_c, above[:halo]], axis=0)
    inter_all = jnp.concatenate([below[halo:], inter_c, above[halo:]], axis=0)
    up_e = inter_all[1:]
    down_e = inter_all[:-1]

    cond_rows, cond_cols, cond_cross, ply_cosine, ply_sine = ply_tables(angles)
    source_e = tsai_wu(
        strain_e[:, 0][:, None],
        strain_e[:, 1][:, None],
        strain_e[:, 2][:, None],
        ply_cosine,
        ply_sine,
    )
    ply_at = lax.axis_index("ply") * ply_local - halo + jnp.arange(ply_local + 2 * halo)
    col_at = lax.axis_index("tile") * col_local - halo + jnp.arange(width)
    inside = (
        ((ply_at >= 0) & (ply_at < ply_local * ply_count))[:, None, None]
        & ((col_at >= 0) & (col_at < col_local * tile_count))[None, None, :]
    ).astype(jnp.float32)

    diagonal_sum = 2.0 * cond_rows + 2.0 * cond_cols + up_e + down_e + stiff_e
    adjoint = relaxation * source_e / diagonal_sum * inside
    for iteration in range(1, ITERS - 1):
        adjoint = sweep(
            jnp.pad(adjoint, ((0, 0), (1, 1), (0, 0), (1, 1))),
            source_e,
            stiff_e,
            up_e,
            down_e,
            cond_rows,
            cond_cols,
            cond_cross,
        )
        adjoint = adjoint * inside
    adjoint = sweep(
        trim(adjoint, halo - 1, 1, 3),
        trim(source_e, halo, 1, 3),
        trim(stiff_e, halo, 0, 2),
        trim(up_e, halo, 0, 2),
        trim(down_e, halo, 0, 2),
        cond_rows[halo : cond_rows.shape[0] - halo],
        cond_cols[halo : cond_cols.shape[0] - halo],
        cond_cross[halo : cond_cross.shape[0] - halo],
    )
    source = trim(source_e, halo, 1, 3)
    product = adjoint * source
    total = jnp.sum(product, axis=(0, 1))
    totals = lax.all_to_all(
        jnp.broadcast_to(total[None], (ply_count,) + total.shape), "ply", 0, 0, tiled=True
    )
    lower = (jnp.arange(ply_count) < lax.axis_index("ply")).astype(jnp.float32)
    prefix = jnp.sum(totals * lower[:, None, None], axis=0)
    running = jnp.cumsum(jnp.sum(product, axis=0), axis=0)
    through = (running + prefix[None]) / (ply_local * ply_count)
    return (adjoint, through)


def solution(mesh):
    return jax.shard_map(
        body,
        mesh=mesh,
        in_specs=(
            P(None, None, None, "tile"),
            P(),
            P("ply"),
            P("ply", None, "tile"),
            P("ply", None, "tile"),
        ),
        out_specs=(P(None, "ply", None, "tile"), P("ply", None, "tile")),
        check_vma=False,
    )
```

```python
import jax
import jax.numpy as jnp
from jax import lax
from jax.sharding import PartitionSpec as P
from jax.experimental import pallas as pl
from jax.experimental.pallas import tpu as pltpu

ITERS = 4


relaxation = 2.0 / 3.0
half_root = 0.7071067811865476
fibre_modulus = 1.0
trans_modulus = 0.5
shear_modulus = 0.3
linear_fibre = 0.3
linear_trans = 0.8
square_fibre = 0.5
square_trans = 1.0
square_shear = 0.8
cross_term = -0.35


def passed_along(array, axis, by):
    count = lax.axis_size(axis)
    pairs = [(i, i + by) for i in range(count) if 0 <= i + by < count]
    return lax.ppermute(array, axis, pairs)


def with_halos(block, axis, dim, below, above):
    size = block.shape[dim]
    low = passed_along(lax.slice_in_dim(block, size - below, size, axis=dim), axis, 1)
    high = passed_along(lax.slice_in_dim(block, 0, above, axis=dim), axis, -1)
    return jnp.concatenate([low, block, high], axis=dim)


def ply_tables(angles):
    one_hot = (angles[:, None] == jnp.arange(4, dtype=jnp.int32)[None, :]).astype(jnp.float32)
    ply_cosine = jnp.sum(
        one_hot * jnp.array([1.0, half_root, half_root, 0.0], jnp.float32)[None, :], axis=1
    )
    ply_sine = jnp.sum(
        one_hot * jnp.array([0.0, half_root, -half_root, 1.0], jnp.float32)[None, :], axis=1
    )
    ply_cosine = ply_cosine.reshape(-1, 1, 1)
    ply_sine = ply_sine.reshape(-1, 1, 1)
    cond_rows = 4.0 * ply_cosine * ply_cosine + ply_sine * ply_sine
    cond_cols = 4.0 * ply_sine * ply_sine + ply_cosine * ply_cosine
    cond_cross = 3.0 * ply_cosine * ply_sine
    return (cond_rows, cond_cols, cond_cross, ply_cosine, ply_sine)


def tsai_wu(strain_x, strain_y, strain_xy, ply_cosine, ply_sine):
    cos_sq = ply_cosine * ply_cosine
    sin_sq = ply_sine * ply_sine
    mixed = ply_cosine * ply_sine
    fibre_strain = cos_sq * strain_x + sin_sq * strain_y + mixed * strain_xy
    trans_strain = sin_sq * strain_x + cos_sq * strain_y - mixed * strain_xy
    shear_strain = 2.0 * mixed * (strain_y - strain_x) + (cos_sq - sin_sq) * strain_xy
    fibre_stress = fibre_modulus * fibre_strain
    trans_stress = trans_modulus * trans_strain
    shear_stress = shear_modulus * shear_strain
    first = linear_fibre + 2.0 * square_fibre * fibre_stress + 2.0 * cross_term * trans_stress
    second = linear_trans + 2.0 * square_trans * trans_stress + 2.0 * cross_term * fibre_stress
    return first + second + 2.0 * square_shear * shear_stress


def sweep(padded, source, stiffening, coupling_up, coupling_down, cond_rows, cond_cols, cond_cross):
    widths = [(0, 0)] * (padded.ndim - 2) + [(1, 1), (0, 0)]
    framed = jnp.pad(padded, widths)
    centre = framed[..., 1:-1, 1:-1, 1:-1]
    along_rows = framed[..., 1:-1, 2:, 1:-1] + framed[..., 1:-1, :-2, 1:-1]
    along_cols = framed[..., 1:-1, 1:-1, 2:] + framed[..., 1:-1, 1:-1, :-2]
    diagonal_pairs = (
        framed[..., 1:-1, 2:, 2:]
        + framed[..., 1:-1, :-2, :-2]
        - framed[..., 1:-1, 2:, :-2]
        - framed[..., 1:-1, :-2, 2:]
    )
    overhead = framed[..., 2:, 1:-1, 1:-1]
    beneath = framed[..., :-2, 1:-1, 1:-1]
    image = (
        cond_rows * (2.0 * centre - along_rows)
        + cond_cols * (2.0 * centre - along_cols)
        - 0.5 * cond_cross * diagonal_pairs
    )
    image = (
        image
        + coupling_up * (centre - overhead)
        + coupling_down * (centre - beneath)
        + stiffening * centre
    )
    diagonal_sum = 2.0 * cond_rows + 2.0 * cond_cols + coupling_up + coupling_down + stiffening
    return centre + relaxation * (source - image) / diagonal_sum


def sweeps_kernel(
    tab, ply_mask, strain_ref, stiff_ref, inter_ref, col_mask_ref, adj_ref, acc_ref,
    src_s, forced_s, scale_s, up_s, down_s, a_s, b_s,
):
    case = pl.program_id(0)
    planes, rows, lanes = stiff_ref.shape
    halo = ITERS - 1
    own_planes, own_cols = acc_ref.shape[0], acc_ref.shape[2]
    col_mask = col_mask_ref[...]
    row = lax.broadcasted_iota(jnp.int32, (rows, lanes), 0)
    keep_a = (jnp.abs(pltpu.roll(row, 1, 0) - row) == 1).astype(jnp.float32)
    keep_b = (jnp.abs(pltpu.roll(row, rows - 1, 0) - row) == 1).astype(jnp.float32)
    strain_x = strain_ref[0, 0]
    strain_y = strain_ref[0, 1]
    strain_xy = strain_ref[0, 2]

    def diagonal_at(p):
        cond_rows, cond_cols = tab[0, p], tab[1, p]
        return 2.0 * cond_rows + 2.0 * cond_cols + inter_ref[p + 1] + inter_ref[p] + stiff_ref[p]

    @pl.when(case == 0)
    def _():
        def scales(p, carry):
            scale = relaxation / diagonal_at(p)
            scale_s[p] = scale
            up_s[p] = scale * inter_ref[p + 1]
            down_s[p] = scale * inter_ref[p]
            return carry

        lax.fori_loop(0, planes, scales, 0)
        acc_ref[...] = jnp.zeros(acc_ref.shape, jnp.float32)

    def first(p, carry):
        source = tsai_wu(strain_x, strain_y, strain_xy, tab[3, p], tab[4, p])
        forced = relaxation * source / diagonal_at(p)
        src_s[p] = source
        forced_s[p] = forced
        a_s[p] = forced * (ply_mask[p] * col_mask)
        return carry

    lax.fori_loop(0, planes, first, 0, unroll=2)
    buffers = (a_s, b_s)
    for iteration in range(1, ITERS):
        previous, following = buffers[(iteration - 1) % 2], buffers[iteration % 2]
        masked = iteration < ITERS - 1

        def step(p, carry, previous=previous, following=following, masked=masked):
            centre = previous[p]
            row_a = pltpu.roll(centre, 1, 0) * keep_a
            row_b = pltpu.roll(centre, rows - 1, 0) * keep_b
            along_rows = row_a + row_b
            along_cols = pltpu.roll(centre, 1, 1) + pltpu.roll(centre, lanes - 1, 1)
            diagonal_pairs = (
                pltpu.roll(row_a, 1, 1)
                + pltpu.roll(row_b, lanes - 1, 1)
                - pltpu.roll(row_a, lanes - 1, 1)
                - pltpu.roll(row_b, 1, 1)
            )
            in_plane = (
                tab[0, p] * along_rows + tab[1, p] * along_cols + (0.5 * tab[2, p]) * diagonal_pairs
            )
            value = (
                (1.0 - relaxation) * centre
                + forced_s[p]
                + scale_s[p] * in_plane
                + up_s[p] * previous[p + 1]
                + down_s[p] * previous[p - 1]
            )
            if masked:
                following[p] = value * (ply_mask[p] * col_mask)
            else:
                value = value[:, :own_cols]
                adj_ref[0, p - halo] = value
                acc_ref[p - halo] = acc_ref[p - halo] + value * src_s[p][:, :own_cols]
            return carry

        lax.fori_loop(iteration, planes - iteration, step, 0, unroll=2)


def trim(array, by, ply_dim, col_dim):
    if by == 0:
        return array
    array = lax.slice_in_dim(array, by, array.shape[ply_dim] - by, axis=ply_dim)
    return lax.slice_in_dim(array, by, array.shape[col_dim] - by, axis=col_dim)


def body(strain, case_ids, angle_ids, stiffening, interface):
    halo = ITERS - 1
    ply_local = angle_ids.shape[0]
    col_local = stiffening.shape[2]
    ply_count = lax.axis_size("ply")
    tile_count = lax.axis_size("tile")
    cases = case_ids.shape[0]
    rows = strain.shape[2]
    lanes = -(-(col_local + 2 * halo) // 128) * 128

    def edge(start):
        return jnp.concatenate(
            [
                lax.slice_in_dim(strain, start, start + halo, axis=3).reshape(-1, rows, halo),
                lax.slice_in_dim(stiffening, start, start + halo, axis=2),
                lax.slice_in_dim(interface, start, start + halo, axis=2),
            ],
            axis=0,
        )

    left = passed_along(edge(col_local - halo), "tile", 1)
    right = passed_along(edge(0), "tile", -1)
    states = strain.shape[0] * 3

    def circular(own, first, last):
        gap = jnp.zeros(own.shape[:-1] + (lanes - col_local - 2 * halo,), jnp.float32)
        return jnp.concatenate([own, right[first:last].reshape(own.shape[:-1] + (halo,)), gap,
                                left[first:last].reshape(own.shape[:-1] + (halo,))], axis=-1)

    strain_e = jnp.take(circular(strain, 0, states), case_ids, axis=0)
    stiff_c = circular(stiffening, states, states + ply_local)
    inter_c = circular(interface, states + ply_local, states + 2 * ply_local)
    angle_plane = jnp.zeros((1, rows, lanes), jnp.float32)
    below = passed_along(
        jnp.concatenate(
            [
                stiff_c[ply_local - halo :],
                inter_c[ply_local - halo - 1 :],
                angle_plane.at[0, 0, :halo].set(angle_ids[ply_local - halo :].astype(jnp.float32)),
            ],
            axis=0,
        ),
        "ply",
        1,
    )
    above = passed_along(
        jnp.concatenate(
            [
                stiff_c[:halo],
                inter_c[:halo],
                angle_plane.at[0, 0, :halo].set(angle_ids[:halo].astype(jnp.float32)),
            ],
            axis=0,
        ),
        "ply",
        -1,
    )
    angles = jnp.concatenate(
        [
            below[2 * halo + 1, 0, :halo].astype(jnp.int32),
            angle_ids,
            above[2 * halo, 0, :halo].astype(jnp.int32),
        ]
    )
    stiff_e = jnp.concatenate([below[:halo], stiff_c, above[:halo]], axis=0)
    inter_all = jnp.concatenate([below[halo : 2 * halo + 1], inter_c, above[halo : 2 * halo]], axis=0)

    cond_rows, cond_cols, cond_cross, ply_cosine, ply_sine = ply_tables(angles)
    tab = jnp.stack(
        [t.reshape(-1) for t in (cond_rows, cond_cols, cond_cross, ply_cosine, ply_sine)]
    )
    planes = ply_local + 2 * halo
    ply_at = lax.axis_index("ply") * ply_local - halo + jnp.arange(planes)
    ply_mask = ((ply_at >= 0) & (ply_at < ply_local * ply_count)).astype(jnp.float32)
    lane = jnp.arange(lanes)
    col_at = lax.axis_index("tile") * col_local + jnp.where(lane >= lanes - halo, lane - lanes, lane)
    col_ok = (lane < col_local + halo) | (lane >= lanes - halo)
    col_ok = col_ok & (col_at >= 0) & (col_at < col_local * tile_count)
    col_mask = jnp.broadcast_to(col_ok.astype(jnp.float32)[None, :], (rows, lanes))

    adjoint, summed = pl.pallas_call(
        sweeps_kernel,
        grid=(cases,),
        in_specs=[
            pl.BlockSpec(memory_space=pltpu.SMEM),
            pl.BlockSpec(memory_space=pltpu.SMEM),
            pl.BlockSpec((1, 3, rows, lanes), lambda c: (c, 0, 0, 0)),
            pl.BlockSpec((planes, rows, lanes), lambda c: (0, 0, 0)),
            pl.BlockSpec((planes + 1, rows, lanes), lambda c: (0, 0, 0)),
            pl.BlockSpec((rows, lanes), lambda c: (0, 0)),
        ],
        out_specs=[
            pl.BlockSpec((1, ply_local, rows, col_local), lambda c: (c, 0, 0, 0)),
            pl.BlockSpec((ply_local, rows, col_local), lambda c: (0, 0, 0)),
        ],
        out_shape=[
            jax.ShapeDtypeStruct((cases, ply_local, rows, col_local), jnp.float32),
            jax.ShapeDtypeStruct((ply_local, rows, col_local), jnp.float32),
        ],
        scratch_shapes=[pltpu.VMEM((planes, rows, lanes), jnp.float32)] * 7,
        compiler_params=pltpu.CompilerParams(dimension_semantics=("arbitrary",)),
    )(tab, ply_mask, strain_e, stiff_e, inter_all, col_mask)
    total = jnp.sum(summed, axis=0)
    totals = lax.all_to_all(
        jnp.broadcast_to(total[None], (ply_count,) + total.shape), "ply", 0, 0, tiled=True
    )
    lower = (jnp.arange(ply_count) < lax.axis_index("ply")).astype(jnp.float32)
    prefix = jnp.sum(totals * lower[:, None, None], axis=0)
    running = jnp.cumsum(summed, axis=0)
    through = (running + prefix[None]) / (ply_local * ply_count)
    return (adjoint, through)


def solution(mesh):
    return jax.shard_map(
        body,
        mesh=mesh,
        in_specs=(
            P(None, None, None, "tile"),
            P(),
            P("ply"),
            P("ply", None, "tile"),
            P("ply", None, "tile"),
        ),
        out_specs=(P(None, "ply", None, "tile"), P("ply", None, "tile")),
        check_vma=False,
    )
```

```python
import jax
import jax.numpy as jnp
from jax import lax
from jax.sharding import PartitionSpec as P

ITERS = 4


relaxation = 2.0 / 3.0
half_root = 0.7071067811865476
fibre_modulus = 1.0
trans_modulus = 0.5
shear_modulus = 0.3
linear_fibre = 0.3
linear_trans = 0.8
square_fibre = 0.5
square_trans = 1.0
square_shear = 0.8
cross_term = -0.35


def passed_along(array, axis, by):
    count = lax.axis_size(axis)
    pairs = [(i, i + by) for i in range(count) if 0 <= i + by < count]
    return lax.ppermute(array, axis, pairs)


def with_halos(block, axis, dim, below, above):
    size = block.shape[dim]
    low = passed_along(lax.slice_in_dim(block, size - below, size, axis=dim), axis, 1)
    high = passed_along(lax.slice_in_dim(block, 0, above, axis=dim), axis, -1)
    return jnp.concatenate([low, block, high], axis=dim)


def ply_tables(angles):
    one_hot = (angles[:, None] == jnp.arange(4, dtype=jnp.int32)[None, :]).astype(jnp.float32)
    ply_cosine = jnp.sum(
        one_hot * jnp.array([1.0, half_root, half_root, 0.0], jnp.float32)[None, :], axis=1
    )
    ply_sine = jnp.sum(
        one_hot * jnp.array([0.0, half_root, -half_root, 1.0], jnp.float32)[None, :], axis=1
    )
    ply_cosine = ply_cosine.reshape(-1, 1, 1)
    ply_sine = ply_sine.reshape(-1, 1, 1)
    cond_rows = 4.0 * ply_cosine * ply_cosine + ply_sine * ply_sine
    cond_cols = 4.0 * ply_sine * ply_sine + ply_cosine * ply_cosine
    cond_cross = 3.0 * ply_cosine * ply_sine
    return (cond_rows, cond_cols, cond_cross, ply_cosine, ply_sine)


def tsai_wu(strain_x, strain_y, strain_xy, ply_cosine, ply_sine):
    cos_sq = ply_cosine * ply_cosine
    sin_sq = ply_sine * ply_sine
    mixed = ply_cosine * ply_sine
    fibre_strain = cos_sq * strain_x + sin_sq * strain_y + mixed * strain_xy
    trans_strain = sin_sq * strain_x + cos_sq * strain_y - mixed * strain_xy
    shear_strain = 2.0 * mixed * (strain_y - strain_x) + (cos_sq - sin_sq) * strain_xy
    fibre_stress = fibre_modulus * fibre_strain
    trans_stress = trans_modulus * trans_strain
    shear_stress = shear_modulus * shear_strain
    first = linear_fibre + 2.0 * square_fibre * fibre_stress + 2.0 * cross_term * trans_stress
    second = linear_trans + 2.0 * square_trans * trans_stress + 2.0 * cross_term * fibre_stress
    return first + second + 2.0 * square_shear * shear_stress


def sweep(padded, source, stiffening, coupling_up, coupling_down, cond_rows, cond_cols, cond_cross):
    widths = [(0, 0)] * (padded.ndim - 2) + [(1, 1), (0, 0)]
    framed = jnp.pad(padded, widths)
    centre = framed[..., 1:-1, 1:-1, 1:-1]
    along_rows = framed[..., 1:-1, 2:, 1:-1] + framed[..., 1:-1, :-2, 1:-1]
    along_cols = framed[..., 1:-1, 1:-1, 2:] + framed[..., 1:-1, 1:-1, :-2]
    diagonal_pairs = (
        framed[..., 1:-1, 2:, 2:]
        + framed[..., 1:-1, :-2, :-2]
        - framed[..., 1:-1, 2:, :-2]
        - framed[..., 1:-1, :-2, 2:]
    )
    overhead = framed[..., 2:, 1:-1, 1:-1]
    beneath = framed[..., :-2, 1:-1, 1:-1]
    image = (
        cond_rows * (2.0 * centre - along_rows)
        + cond_cols * (2.0 * centre - along_cols)
        - 0.5 * cond_cross * diagonal_pairs
    )
    image = (
        image
        + coupling_up * (centre - overhead)
        + coupling_down * (centre - beneath)
        + stiffening * centre
    )
    diagonal_sum = 2.0 * cond_rows + 2.0 * cond_cols + coupling_up + coupling_down + stiffening
    return centre + relaxation * (source - image) / diagonal_sum


def trim(array, by, ply_dim, col_dim):
    if by == 0:
        return array
    array = lax.slice_in_dim(array, by, array.shape[ply_dim] - by, axis=ply_dim)
    return lax.slice_in_dim(array, by, array.shape[col_dim] - by, axis=col_dim)


def body(strain, case_ids, angle_ids, stiffening, interface):
    halo = ITERS - 1
    ply_local = angle_ids.shape[0]
    col_local = stiffening.shape[2]
    ply_count = lax.axis_size("ply")
    tile_count = lax.axis_size("tile")
    cases = case_ids.shape[0]
    rows = strain.shape[2]
    width = col_local + 2 * halo

    angle_plane = jnp.zeros((1, rows, col_local), jnp.float32)
    below = passed_along(
        jnp.concatenate(
            [
                stiffening[ply_local - halo :],
                interface[ply_local - halo - 1 :],
                angle_plane.at[0, 0, :halo].set(angle_ids[ply_local - halo :].astype(jnp.float32)),
            ],
            axis=0,
        ),
        "ply",
        1,
    )
    above = passed_along(
        jnp.concatenate(
            [
                stiffening[:halo],
                interface[:halo],
                angle_plane.at[0, 0, :halo].set(angle_ids[:halo].astype(jnp.float32)),
            ],
            axis=0,
        ),
        "ply",
        -1,
    )
    angles = jnp.concatenate(
        [
            below[2 * halo + 1, 0, :halo].astype(jnp.int32),
            angle_ids,
            above[2 * halo, 0, :halo].astype(jnp.int32),
        ]
    )
    stiff_p = jnp.concatenate([below[:halo], stiffening, above[:halo]], axis=0)
    inter_p = jnp.concatenate([below[halo : 2 * halo + 1], interface, above[halo : 2 * halo]], axis=0)

    def edge(start):
        return jnp.concatenate(
            [
                lax.slice_in_dim(strain, start, start + halo, axis=3).reshape(-1, rows, halo),
                lax.slice_in_dim(stiff_p, start, start + halo, axis=2),
                lax.slice_in_dim(inter_p, start, start + halo, axis=2),
            ],
            axis=0,
        )

    left = passed_along(edge(col_local - halo), "tile", 1)
    right = passed_along(edge(0), "tile", -1)
    states = strain.shape[0] * 3
    strain_all = jnp.concatenate(
        [
            left[:states].reshape(strain.shape[:3] + (halo,)),
            strain,
            right[:states].reshape(strain.shape[:3] + (halo,)),
        ],
        axis=3,
    )
    strain_e = jnp.take(strain_all, case_ids, axis=0)
    split = states + stiff_p.shape[0]
    stiff_e = jnp.concatenate([left[states:split], stiff_p, right[states:split]], axis=2)
    inter_all = jnp.concatenate([left[split:], inter_p, right[split:]], axis=2)
    up_e = inter_all[1:]
    down_e = inter_all[:-1]

    cond_rows, cond_cols, cond_cross, ply_cosine, ply_sine = ply_tables(angles)
    source_e = tsai_wu(
        strain_e[:, 0][:, None],
        strain_e[:, 1][:, None],
        strain_e[:, 2][:, None],
        ply_cosine,
        ply_sine,
    )
    ply_at = lax.axis_index("ply") * ply_local - halo + jnp.arange(ply_local + 2 * halo)
    col_at = lax.axis_index("tile") * col_local - halo + jnp.arange(width)
    inside = (
        ((ply_at >= 0) & (ply_at < ply_local * ply_count))[:, None, None]
        & ((col_at >= 0) & (col_at < col_local * tile_count))[None, None, :]
    ).astype(jnp.float32)

    diagonal_sum = 2.0 * cond_rows + 2.0 * cond_cols + up_e + down_e + stiff_e
    adjoint = relaxation * source_e / diagonal_sum * inside
    for iteration in range(1, ITERS):
        by = iteration
        adjoint = sweep(
            adjoint,
            trim(source_e, by, 1, 3),
            trim(stiff_e, by, 0, 2),
            trim(up_e, by, 0, 2),
            trim(down_e, by, 0, 2),
            cond_rows[by : cond_rows.shape[0] - by],
            cond_cols[by : cond_cols.shape[0] - by],
            cond_cross[by : cond_cross.shape[0] - by],
        )
        if iteration < ITERS - 1:
            adjoint = adjoint * trim(inside, by, 0, 2)
    source = trim(source_e, halo, 1, 3)
    product = adjoint * source
    total = jnp.sum(product, axis=(0, 1))
    totals = lax.all_to_all(
        jnp.broadcast_to(total[None], (ply_count,) + total.shape), "ply", 0, 0, tiled=True
    )
    lower = (jnp.arange(ply_count) < lax.axis_index("ply")).astype(jnp.float32)
    prefix = jnp.sum(totals * lower[:, None, None], axis=0)
    running = jnp.cumsum(jnp.sum(product, axis=0), axis=0)
    through = (running + prefix[None]) / (ply_local * ply_count)
    return (adjoint, through)


def solution(mesh):
    return jax.shard_map(
        body,
        mesh=mesh,
        in_specs=(
            P(None, None, None, "tile"),
            P(),
            P("ply"),
            P("ply", None, "tile"),
            P("ply", None, "tile"),
        ),
        out_specs=(P(None, "ply", None, "tile"), P("ply", None, "tile")),
        check_vma=False,
    )
```
